128 devices in a mesh: hot: 4 (over z), dom: 32 (over y, x, core).
Axes of the slice: x: 4, y: 4, z: 4, core: 2. Of those that a mesh axis runs over, the one named last changes fastest.
Arguments:
- macro_adjoint: float32 [16, 6], P('hot'), may hold values from -6 to 6
- slip_code: int32 [32, 64, 4096], P('hot', 'dom'), may hold values from 0 to 4095
- grain_id: int32 [32, 64, 4096], P('hot', 'dom'), may hold values from 0 to 63
- grain_modulus: float32 [64], replicated, may hold values from 0.5 to 4
- slip_softening: float32 [64, 12], replicated, may hold values from 0.1 to 1.5
- rve_spot: int32 [32], P('hot'), may hold values from 0 to 15, as said below
Outputs:
- sensitivity: float32 [16, 6], P('hot')
- adjoint_field: float32 [32, 3, 64, 4096], P('hot', None, 'dom')
The draws below stay inside these ranges and needn't reach their ends.
Inputs may be any that keep to these rules, and one draw needn't show every extreme that they name: `rve_spot`: every hot-spot is named by exactly 2 RVEs.
All inputs are finite; a program needn't handle non-finite values.
Results may differ from the reference program's by a relative error of at most 0.0003.
Values sent between devices are 32-bit elements; how exact they have to be, the bound alone decides.
No kernel may reach another device: no remote copies, remote signals or barrier semaphores. Data moves between devices by JAX's collectives and lax.ppermute only.
A program may use at most 64 MiB of HBM per device.

```python
import math
import jax
import jax.numpy as jnp
from jax import lax

RES = 64
SLIPS = 12
GRAINS = 64
ITERS = 8
SPOTS = 16
RVES = 32


def draw_rve_spot(key, part):
    return (jax.random.permutation(key, RVES) // (RVES // SPOTS)).astype(jnp.int32)


def set_ends(drawn, own_key, smallest, high):
    dims = drawn.shape
    spot = [jax.random.randint(jax.random.fold_in(own_key, axis), (), 0, dims[axis]) for axis in range(len(dims))]
    drawn = drawn.at[tuple(spot)].set(smallest)
    longest = dims.index(max(dims))
    spot[longest] = (spot[longest] + 1) % dims[longest]
    return drawn.at[tuple(spot)].set(high)


def level_of(stream_key, dims, split, low, largest):
    def one(dim, parts):
        steps = jax.random.uniform(jax.random.fold_in(jax.random.fold_in(stream_key, 6), dim), (parts,), jnp.float32, low / len(split), largest / len(split))
        return jnp.repeat(jnp.exp(steps), dims[dim] // parts).reshape((-1,) + (1,) * (len(dims) - dim - 1))

    factor_of = one(*split[0])
    for cut in split[1:]:
        factor_of = factor_of * one(*cut)
    return factor_of


def scatter_about(own_key, extent, deviation, limit, cuts=(), kind=jnp.bfloat16):
    entries = deviation * jax.random.normal(own_key, extent, jnp.float32)
    if cuts:
        entries = entries * level_of(own_key, extent, cuts, -0.22, 0.18)
    return jnp.clip(entries, -limit, limit).astype(kind)


def setup_inputs(seed: int = 0) -> dict:
    seeds = jax.random.split(jax.random.key(seed), 7)
    macro_adjoint = scatter_about(seeds[0], (SPOTS, 6), 1.0, 6.0, ((0, 4),), jnp.float32)
    slip_code = set_ends(jax.random.randint(seeds[1], (RVES, RES, RES * RES), 0, 4096), jax.random.fold_in(seeds[1], 1), 0, 4095).astype(jnp.int32)
    grain_id = set_ends(jax.random.randint(seeds[2], (RVES, RES, RES * RES), 0, GRAINS), jax.random.fold_in(seeds[2], 1), 0, GRAINS - 1).astype(jnp.int32)
    grain_modulus = jnp.clip(jnp.exp(jax.random.uniform(seeds[3], (GRAINS,), jnp.float32, math.log(0.5), math.log(4.0))), 0.5, 4.0)
    slip_softening = jnp.clip(jnp.exp(jax.random.uniform(seeds[4], (GRAINS, SLIPS), jnp.float32, math.log(0.1), math.log(1.5))), 0.1, 1.5)
    rve_spot = draw_rve_spot(jax.random.fold_in(seeds[6], 71), 0)
    return dict(macro_adjoint=macro_adjoint, slip_code=slip_code, grain_id=grain_id, grain_modulus=grain_modulus, slip_softening=slip_softening, rve_spot=rve_spot)


mass_term = 0.02


def reference(macro_adjoint, slip_code, grain_id, grain_modulus, slip_softening, rve_spot):
    strains = macro_adjoint[rve_spot]

    def solve_with(inputs):
        return solve_rve_tables(inputs, grain_modulus, slip_softening)

    fields, results = lax.map(solve_with, (slip_code, grain_id, strains))
    totals = jax.ops.segment_sum(results, rve_spot, num_segments=SPOTS) / float(RVES // SPOTS)
    return totals, fields


def solve_rve_tables(inputs, grain_modulus, slip_softening):
    codes, grain_cells, strain_row = inputs
    return solve_core(codes, grain_cells, strain_row, grain_modulus, slip_softening)


def solve_core(codes, grain_cells, strain_row, modulus_table_in, slip_table_in):
    codes = codes.reshape(RES, RES, RES)
    grain_cells = grain_cells.reshape(RES, RES, RES)
    softening = jnp.zeros((RES, RES, RES), jnp.float32)
    for slip in range(SLIPS):
        active = ((codes // (2 ** slip)) % 2).astype(jnp.float32)
        softening = softening + active * slip_table_in[grain_cells, slip]
    stiff = modulus_table_in[grain_cells] / (1.0 + softening)
    padded = jnp.pad(stiff, 1)
    near_xup = padded[2:, 1:-1, 1:-1]
    near_xdn = padded[:-2, 1:-1, 1:-1]
    near_yup = padded[1:-1, 2:, 1:-1]
    near_ydn = padded[1:-1, :-2, 1:-1]
    near_zup = padded[1:-1, 1:-1, 2:]
    near_zdn = padded[1:-1, 1:-1, :-2]
    face_xup = 0.5 * (stiff + near_xup)
    face_xdn = 0.5 * (stiff + near_xdn)
    face_yup = 0.5 * (stiff + near_yup)
    face_ydn = 0.5 * (stiff + near_ydn)
    face_zup = 0.5 * (stiff + near_zup)
    face_zdn = 0.5 * (stiff + near_zdn)
    diagonal_sum = mass_term + face_xup + face_xdn + face_yup + face_ydn + face_zup + face_zdn
    gradients = [0.5 * (near_xup - near_xdn), 0.5 * (near_yup - near_ydn), 0.5 * (near_zup - near_zdn)]
    tensor = [[strain_row[0], strain_row[5], strain_row[4]],
              [strain_row[5], strain_row[1], strain_row[3]],
              [strain_row[4], strain_row[3], strain_row[2]]]
    source = jnp.stack([gradients[0] * tensor[comp][0] + gradients[1] * tensor[comp][1]
                        + gradients[2] * tensor[comp][2] for comp in range(3)])

    def operate(field):
        wide = jnp.pad(field, ((0, 0), (1, 1), (1, 1), (1, 1)))
        return (diagonal_sum * field - face_xup * wide[:, 2:, 1:-1, 1:-1] - face_xdn * wide[:, :-2, 1:-1, 1:-1]
                - face_yup * wide[:, 1:-1, 2:, 1:-1] - face_ydn * wide[:, 1:-1, :-2, 1:-1]
                - face_zup * wide[:, 1:-1, 1:-1, 2:] - face_zdn * wide[:, 1:-1, 1:-1, :-2])

    answer = jnp.zeros_like(source)
    residual = source
    direction = source
    norm_now = jnp.sum(residual * residual)
    for step in range(ITERS):
        image = operate(direction)
        alpha = norm_now / jnp.sum(direction * image)
        answer = answer + alpha * direction
        residual = residual - alpha * image
        norm_next = jnp.sum(residual * residual)
        direction = residual + (norm_next / norm_now) * direction
        norm_now = norm_next
    volume = float(RES ** 3)
    stiff_mean = jnp.sum(stiff) / volume
    moment = [[jnp.sum(answer[comp] * gradients[other]) for other in range(3)] for comp in range(3)]
    pairs = [(0, 0), (1, 1), (2, 2), (1, 2), (0, 2), (0, 1)]
    result = jnp.stack([stiff_mean * strain_row[slot]
                        - 0.5 * (moment[pairs[slot][0]][pairs[slot][1]] + moment[pairs[slot][1]][pairs[slot][0]]) / volume
                        for slot in range(6)])
    return answer.reshape(3, RES, RES * RES), result
```

```python
import jax
import jax.numpy as jnp
from jax import lax
from jax.sharding import PartitionSpec as P

RES = 64
SLIPS = 12
GRAINS = 64
ITERS = 8


mass_term = 0.02


def padded_2(value, sides, width):
    for axis, dim in sides:
        devices, length = (lax.axis_size(axis), value.shape[dim])
        up = [(i, (i + 1) % devices) for i in range(devices - 1)]
        down = [(j, i) for i, j in up]
        last = lax.slice_in_dim(value, length - width, length, axis=dim)
        leading = lax.slice_in_dim(value, 0, width, axis=dim)
        before = lax.ppermute(last, axis, up)
        after = lax.ppermute(leading, axis, down)
        value = jnp.concatenate([before, value, after], axis=dim)
    return value


def xor_groups(size):
    bits = size.bit_length() - 1
    if size != 1 << bits:
        return None
    groups = [(0, 1)] if bits % 2 else []
    lo = bits % 2
    while lo < bits:
        groups.append((lo, 2))
        lo += 2
    return groups


def tree_sum(vals, nb):
    cur = dict(vals)
    for level in range(nb):
        cur = {o: v + cur[o | (1 << level)] for o, v in cur.items() if not o & (1 << level)}
    return cur[0]


def axis_sum(value, axis):
    size = lax.axis_size(axis)
    groups = xor_groups(size)
    if groups is None:
        return lax.psum(value, axis)
    for lo, nb in groups:
        vals = {0: value}
        for o in range(1, 1 << nb):
            mask = o << lo
            vals[o] = lax.ppermute(value, axis, [(i, i ^ mask) for i in range(size)])
        value = tree_sum(vals, nb)
    return value


def axis_gather(value, axis):
    size = lax.axis_size(axis)
    if xor_groups(size) is None:
        return [lax.all_gather(value, axis, axis=0, tiled=True)], None
    parts = [value] + [
        lax.ppermute(value, axis, [(i, i ^ o) for i in range(size)]) for o in range(1, size)
    ]
    return parts, lax.axis_index(axis)


def axis_reduce_scatter(value, axis):
    size = lax.axis_size(axis)
    if xor_groups(size) is None:
        return lax.psum_scatter(value, axis, scatter_dimension=0, tiled=True)
    me = lax.axis_index(axis)
    block = value.shape[0] // size
    nb = size.bit_length() - 1
    vals = {0: lax.dynamic_slice_in_dim(value, me * block, block, 0)}
    for o in range(1, size):
        wanted = lax.dynamic_slice_in_dim(value, (me ^ o) * block, block, 0)
        vals[o] = lax.ppermute(wanted, axis, [(i, i ^ o) for i in range(size)])
    return tree_sum(vals, nb)


def shift_cells(field, step):
    filler = jnp.zeros(field.shape[:-1] + (abs(step),), field.dtype)
    if step > 0:
        return jnp.concatenate([field[..., step:], filler], -1)
    return jnp.concatenate([filler, field[..., :step]], -1)


def local_dot(first, second):
    return jnp.sum(first * second, axis=(1, 2, 3))


def shards(macro_adjoint, slip_code, grain_id, grain_modulus, slip_softening, rve_spot):
    rve_count = slip_code.shape[0]
    cells = slip_code.shape[2]
    spot_count = macro_adjoint.shape[0] * lax.axis_size("hot")
    column = jnp.arange(cells) % RES
    upper_mask = (column != RES - 1).astype(jnp.float32)
    lower_mask = (column != 0).astype(jnp.float32)
    table = jnp.concatenate([grain_modulus[None, :], slip_softening.T], 0)

    def stiff_one(inputs):
        codes, grain_cells = inputs
        flat_codes = codes.reshape(-1)
        flat_grains = grain_cells.reshape(-1)
        onehot = (jnp.arange(GRAINS)[:, None] == flat_grains[None, :]).astype(jnp.float32)
        looked = jnp.dot(
            table, onehot, precision=lax.Precision.HIGHEST, preferred_element_type=jnp.float32
        )
        softening = jnp.zeros(flat_codes.shape, jnp.float32)
        for slip in range(SLIPS):
            active = (flat_codes // 2**slip % 2).astype(jnp.float32)
            softening = softening + active * looked[1 + slip]
        return (looked[0] / (1.0 + softening)).reshape(codes.shape)

    spot_onehot = (rve_spot[:, None] == jnp.arange(spot_count)[None, :]).astype(jnp.float32)
    parts, hot_me = axis_gather(macro_adjoint, "hot")
    if hot_me is None:
        all_strains = parts[0]
    else:
        local = macro_adjoint.shape[0]
        ordered = []
        for j in range(len(parts)):
            pick = [(hot_me ^ o) == j for o in range(len(parts))]
            block = parts[0]
            for o in range(1, len(parts)):
                block = jnp.where(pick[o], parts[o], block)
            ordered.append(block)
        all_strains = jnp.concatenate(ordered, 0)
    strains = jnp.dot(
        spot_onehot,
        all_strains,
        precision=lax.Precision.HIGHEST,
        preferred_element_type=jnp.float32,
    )
    stiff = lax.map(stiff_one, (slip_code, grain_id))
    padded = padded_2(stiff, (("dom", 1),), 1)

    def squares(residual):
        return axis_sum(local_dot(residual, residual), "dom")

    near_xup = padded[:, 2:]
    near_xdn = padded[:, :-2]
    near_yup = shift_cells(stiff, RES)
    near_ydn = shift_cells(stiff, -RES)
    near_zup = shift_cells(stiff, 1) * upper_mask
    near_zdn = shift_cells(stiff, -1) * lower_mask
    face_xup = 0.5 * (stiff + near_xup)
    face_xdn = 0.5 * (stiff + near_xdn)
    face_yup = 0.5 * (stiff + near_yup)
    face_ydn = 0.5 * (stiff + near_ydn)
    face_zup = 0.5 * (stiff + near_zup)
    face_zdn = 0.5 * (stiff + near_zdn)
    diagonal_sum = (mass_term + face_xup + face_xdn + face_yup + face_ydn + face_zup + face_zdn)[
        :, None
    ]
    gradients = [
        0.5 * (near_xup - near_xdn),
        0.5 * (near_yup - near_ydn),
        0.5 * (near_zup - near_zdn),
    ]
    tensor = [
        [strains[:, 0], strains[:, 5], strains[:, 4]],
        [strains[:, 5], strains[:, 1], strains[:, 3]],
        [strains[:, 4], strains[:, 3], strains[:, 2]],
    ]
    source = jnp.stack(
        [
            gradients[0] * tensor[comp][0][:, None, None]
            + gradients[1] * tensor[comp][1][:, None, None]
            + gradients[2] * tensor[comp][2][:, None, None]
            for comp in range(3)
        ],
        1,
    )

    def expand(values):
        return values[:, None, None, None]

    answer = jnp.zeros_like(source)
    residual = source
    direction = source
    norm_now = squares(residual)
    wide = padded_2(direction, (("dom", 2),), 1)
    for step in range(ITERS):
        image = (
            diagonal_sum * direction
            - face_xup[:, None] * wide[:, :, 2:]
            - face_xdn[:, None] * wide[:, :, :-2]
            - face_yup[:, None] * shift_cells(direction, RES)
            - face_ydn[:, None] * shift_cells(direction, -RES)
            - face_zup[:, None] * (shift_cells(direction, 1) * upper_mask)
            - face_zdn[:, None] * (shift_cells(direction, -1) * lower_mask)
        )
        alpha = norm_now / axis_sum(local_dot(direction, image), "dom")
        answer = answer + expand(alpha) * direction
        residual = residual - expand(alpha) * image
        norm_next = squares(residual)
        beta = expand(norm_next / norm_now)
        if step + 1 < ITERS:
            wide_residual = padded_2(residual, (("dom", 2),), 1)
            edges = jnp.concatenate([wide[:, :, :1], wide[:, :, -1:]], 2)
            edges_residual = jnp.concatenate([wide_residual[:, :, :1], wide_residual[:, :, -1:]], 2)
            edges = edges_residual + beta * edges
        direction = residual + beta * direction
        if step + 1 < ITERS:
            wide = jnp.concatenate([edges[:, :, :1], direction, edges[:, :, 1:]], 2)
        norm_now = norm_next
    volume = float(RES**3)
    stiff_part = jnp.sum(stiff, axis=(1, 2)) / volume
    moment = [
        [jnp.sum(answer[:, comp] * gradients[other], axis=(1, 2)) for other in range(3)]
        for comp in range(3)
    ]
    pairs = [(0, 0), (1, 1), (2, 2), (1, 2), (0, 2), (0, 1)]
    partial_here = jnp.stack(
        [
            stiff_part * strains[:, slot]
            - 0.5
            * (moment[pairs[slot][0]][pairs[slot][1]] + moment[pairs[slot][1]][pairs[slot][0]])
            / volume
            for slot in range(6)
        ],
        1,
    )
    per_spot = float(rve_count * lax.axis_size("hot") // spot_count)
    rve_totals = axis_sum(partial_here, "dom")
    spot_local = jnp.dot(
        spot_onehot.T,
        rve_totals,
        precision=lax.Precision.HIGHEST,
        preferred_element_type=jnp.float32,
    )
    owned = axis_reduce_scatter(spot_local, "hot")
    return (owned / per_spot, answer)


def solution(mesh):
    return jax.shard_map(
        shards,
        mesh=mesh,
        in_specs=(P("hot", None), P("hot", "dom", None), P("hot", "dom", None), P(), P(), P("hot")),
        out_specs=(P("hot", None), P("hot", None, "dom", None)),
        check_vma=False,
    )
```

```python
import jax
import jax.numpy as jnp
from jax import lax
from jax.sharding import Mesh, PartitionSpec as P

RES = 64
SLIPS = 12
GRAINS = 64
ITERS = 8
RVES = 32


mass_term = 0.02


def padded_2(value, sides, width):
    for axis, dim in sides:
        devices, length = (lax.axis_size(axis), value.shape[dim])
        up = [(i, (i + 1) % devices) for i in range(devices - 1)]
        down = [(j, i) for i, j in up]
        last = lax.slice_in_dim(value, length - width, length, axis=dim)
        leading = lax.slice_in_dim(value, 0, width, axis=dim)
        before = lax.ppermute(last, axis, up)
        after = lax.ppermute(leading, axis, down)
        value = jnp.concatenate([before, value, after], axis=dim)
    return value


def xor_groups(size):
    bits = size.bit_length() - 1
    if size != 1 << bits:
        return None
    groups = [(0, 1)] if bits % 2 else []
    lo = bits % 2
    while lo < bits:
        groups.append((lo, 2))
        lo += 2
    return groups


def tree_sum(vals, nb):
    cur = dict(vals)
    for level in range(nb):
        cur = {o: v + cur[o | (1 << level)] for o, v in cur.items() if not o & (1 << level)}
    return cur[0]


def axis_sum(value, axis):
    size = lax.axis_size(axis)
    groups = xor_groups(size)
    if groups is None:
        return lax.psum(value, axis)
    for lo, nb in groups:
        vals = {0: value}
        for o in range(1, 1 << nb):
            mask = o << lo
            vals[o] = lax.ppermute(value, axis, [(i, i ^ mask) for i in range(size)])
        value = tree_sum(vals, nb)
    return value


def axis_gather(value, axis):
    size = lax.axis_size(axis)
    if xor_groups(size) is None:
        return [lax.all_gather(value, axis, axis=0, tiled=True)], None
    parts = [value] + [
        lax.ppermute(value, axis, [(i, i ^ o) for i in range(size)]) for o in range(1, size)
    ]
    return parts, lax.axis_index(axis)


def axis_reduce_scatter(value, axis):
    size = lax.axis_size(axis)
    if xor_groups(size) is None:
        return lax.psum_scatter(value, axis, scatter_dimension=0, tiled=True)
    me = lax.axis_index(axis)
    block = value.shape[0] // size
    nb = size.bit_length() - 1
    vals = {0: lax.dynamic_slice_in_dim(value, me * block, block, 0)}
    for o in range(1, size):
        wanted = lax.dynamic_slice_in_dim(value, (me ^ o) * block, block, 0)
        vals[o] = lax.ppermute(wanted, axis, [(i, i ^ o) for i in range(size)])
    return tree_sum(vals, nb)


def shift_cells(field, step):
    filler = jnp.zeros(field.shape[:-1] + (abs(step),), field.dtype)
    if step > 0:
        return jnp.concatenate([field[..., step:], filler], -1)
    return jnp.concatenate([filler, field[..., :step]], -1)


def local_dot(first, second):
    return jnp.sum(first * second, axis=(1, 2, 3))


def shards(macro_adjoint, slip_code, grain_id, grain_modulus, slip_softening, rve_spot):
    rve_count = slip_code.shape[0]
    cells = slip_code.shape[2]
    spot_count = macro_adjoint.shape[0] * lax.axis_size("hot")
    column = jnp.arange(cells) % RES
    upper_mask = (column != RES - 1).astype(jnp.float32)
    lower_mask = (column != 0).astype(jnp.float32)
    table = jnp.concatenate([grain_modulus[None, :], slip_softening.T], 0)

    def stiff_one(inputs):
        codes, grain_cells = inputs
        flat_codes = codes.reshape(-1)
        flat_grains = grain_cells.reshape(-1)
        onehot = (jnp.arange(GRAINS)[:, None] == flat_grains[None, :]).astype(jnp.float32)
        looked = jnp.dot(
            table, onehot, precision=lax.Precision.HIGHEST, preferred_element_type=jnp.float32
        )
        softening = jnp.zeros(flat_codes.shape, jnp.float32)
        for slip in range(SLIPS):
            active = (flat_codes // 2**slip % 2).astype(jnp.float32)
            softening = softening + active * looked[1 + slip]
        return (looked[0] / (1.0 + softening)).reshape(codes.shape)

    spot_onehot = (rve_spot[:, None] == jnp.arange(spot_count)[None, :]).astype(jnp.float32)
    parts, hot_me = axis_gather(macro_adjoint, "hot")
    if hot_me is None:
        all_strains = parts[0]
    else:
        local = macro_adjoint.shape[0]
        ordered = []
        for j in range(len(parts)):
            pick = [(hot_me ^ o) == j for o in range(len(parts))]
            block = parts[0]
            for o in range(1, len(parts)):
                block = jnp.where(pick[o], parts[o], block)
            ordered.append(block)
        all_strains = jnp.concatenate(ordered, 0)
    strains = jnp.dot(
        spot_onehot,
        all_strains,
        precision=lax.Precision.HIGHEST,
        preferred_element_type=jnp.float32,
    )
    stiff_slabs = lax.map(stiff_one, (slip_code, grain_id))
    stiff = lax.all_to_all(stiff_slabs, "xc", 0, 1, tiled=True)
    mine = lax.axis_index("xc")
    strains = lax.dynamic_slice_in_dim(strains, mine, 1, 0)
    padded = padded_2(stiff, (("yb", 1),), 1)

    def squares(residual):
        return axis_sum(local_dot(residual, residual), "yb")

    near_xup = padded[:, 2:]
    near_xdn = padded[:, :-2]
    near_yup = shift_cells(stiff, RES)
    near_ydn = shift_cells(stiff, -RES)
    near_zup = shift_cells(stiff, 1) * upper_mask
    near_zdn = shift_cells(stiff, -1) * lower_mask
    face_xup = 0.5 * (stiff + near_xup)
    face_xdn = 0.5 * (stiff + near_xdn)
    face_yup = 0.5 * (stiff + near_yup)
    face_ydn = 0.5 * (stiff + near_ydn)
    face_zup = 0.5 * (stiff + near_zup)
    face_zdn = 0.5 * (stiff + near_zdn)
    diagonal_sum = (mass_term + face_xup + face_xdn + face_yup + face_ydn + face_zup + face_zdn)[
        :, None
    ]
    gradients = [
        0.5 * (near_xup - near_xdn),
        0.5 * (near_yup - near_ydn),
        0.5 * (near_zup - near_zdn),
    ]
    tensor = [
        [strains[:, 0], strains[:, 5], strains[:, 4]],
        [strains[:, 5], strains[:, 1], strains[:, 3]],
        [strains[:, 4], strains[:, 3], strains[:, 2]],
    ]
    source = jnp.stack(
        [
            gradients[0] * tensor[comp][0][:, None, None]
            + gradients[1] * tensor[comp][1][:, None, None]
            + gradients[2] * tensor[comp][2][:, None, None]
            for comp in range(3)
        ],
        1,
    )

    def expand(values):
        return values[:, None, None, None]

    answer = jnp.zeros_like(source)
    residual = source
    direction = source
    norm_now = squares(residual)
    wide = padded_2(direction, (("yb", 2),), 1)
    for step in range(ITERS):
        image = (
            diagonal_sum * direction
            - face_xup[:, None] * wide[:, :, 2:]
            - face_xdn[:, None] * wide[:, :, :-2]
            - face_yup[:, None] * shift_cells(direction, RES)
            - face_ydn[:, None] * shift_cells(direction, -RES)
            - face_zup[:, None] * (shift_cells(direction, 1) * upper_mask)
            - face_zdn[:, None] * (shift_cells(direction, -1) * lower_mask)
        )
        alpha = norm_now / axis_sum(local_dot(direction, image), "yb")
        answer = answer + expand(alpha) * direction
        residual = residual - expand(alpha) * image
        norm_next = squares(residual)
        beta = expand(norm_next / norm_now)
        if step + 1 < ITERS:
            wide_residual = padded_2(residual, (("yb", 2),), 1)
            edges = jnp.concatenate([wide[:, :, :1], wide[:, :, -1:]], 2)
            edges_residual = jnp.concatenate([wide_residual[:, :, :1], wide_residual[:, :, -1:]], 2)
            edges = edges_residual + beta * edges
        direction = residual + beta * direction
        if step + 1 < ITERS:
            wide = jnp.concatenate([edges[:, :, :1], direction, edges[:, :, 1:]], 2)
        norm_now = norm_next
    volume = float(RES**3)
    stiff_part = jnp.sum(stiff, axis=(1, 2)) / volume
    moment = [
        [jnp.sum(answer[:, comp] * gradients[other], axis=(1, 2)) for other in range(3)]
        for comp in range(3)
    ]
    pairs = [(0, 0), (1, 1), (2, 2), (1, 2), (0, 2), (0, 1)]
    partial_here = jnp.stack(
        [
            stiff_part * strains[:, slot]
            - 0.5
            * (moment[pairs[slot][0]][pairs[slot][1]] + moment[pairs[slot][1]][pairs[slot][0]])
            / volume
            for slot in range(6)
        ],
        1,
    )
    per_spot = float(rve_count * lax.axis_size("hot") // spot_count)
    rve_one = axis_sum(partial_here, "yb")
    placed = (jnp.arange(rve_count)[:, None] == mine).astype(jnp.float32) * rve_one
    rve_totals = axis_sum(placed, "xc")
    spot_local = jnp.dot(
        spot_onehot.T,
        rve_totals,
        precision=lax.Precision.HIGHEST,
        preferred_element_type=jnp.float32,
    )
    owned = axis_reduce_scatter(spot_local, "hot")
    return (owned / per_spot, lax.all_to_all(answer, "xc", 2, 0, tiled=True))


def solution(mesh):
    hot, dom = mesh.shape["hot"], mesh.shape["dom"]
    rves_here = RVES // hot
    grouped = Mesh(mesh.devices.reshape(hot, dom // rves_here, rves_here), ("hot", "yb", "xc"))
    return jax.shard_map(
        shards,
        mesh=grouped,
        in_specs=(
            P("hot", None),
            P("hot", ("yb", "xc"), None),
            P("hot", ("yb", "xc"), None),
            P(),
            P(),
            P("hot"),
        ),
        out_specs=(P("hot", None), P("hot", None, ("yb", "xc"), None)),
        check_vma=False,
    )
```

```python
import jax
import jax.numpy as jnp
from jax import lax
from jax.sharding import Mesh, PartitionSpec as P

RES = 64
SLIPS = 12
GRAINS = 64
ITERS = 8
RVES = 32


mass_term = 0.02


def padded_2(value, sides, width):
    for axis, dim in sides:
        devices, length = (lax.axis_size(axis), value.shape[dim])
        up = [(i, (i + 1) % devices) for i in range(devices - 1)]
        down = [(j, i) for i, j in up]
        last = lax.slice_in_dim(value, length - width, length, axis=dim)
        leading = lax.slice_in_dim(value, 0, width, axis=dim)
        before = lax.ppermute(last, axis, up)
        after = lax.ppermute(leading, axis, down)
        value = jnp.concatenate([before, value, after], axis=dim)
    return value


def xor_groups(size):
    bits = size.bit_length() - 1
    if size != 1 << bits:
        return None
    groups = [(0, 1)] if bits % 2 else []
    lo = bits % 2
    while lo < bits:
        groups.append((lo, 2))
        lo += 2
    return groups


def tree_sum(vals, nb):
    cur = dict(vals)
    for level in range(nb):
        cur = {o: v + cur[o | (1 << level)] for o, v in cur.items() if not o & (1 << level)}
    return cur[0]


def axis_sum(value, axis):
    size = lax.axis_size(axis)
    groups = xor_groups(size)
    if groups is None:
        return lax.psum(value, axis)
    for lo, nb in groups:
        vals = {0: value}
        for o in range(1, 1 << nb):
            mask = o << lo
            vals[o] = lax.ppermute(value, axis, [(i, i ^ mask) for i in range(size)])
        value = tree_sum(vals, nb)
    return value


def axis_gather(value, axis):
    size = lax.axis_size(axis)
    if xor_groups(size) is None:
        return [lax.all_gather(value, axis, axis=0, tiled=True)], None
    parts = [value] + [
        lax.ppermute(value, axis, [(i, i ^ o) for i in range(size)]) for o in range(1, size)
    ]
    return parts, lax.axis_index(axis)


def axis_reduce_scatter(value, axis):
    size = lax.axis_size(axis)
    if xor_groups(size) is None:
        return lax.psum_scatter(value, axis, scatter_dimension=0, tiled=True)
    me = lax.axis_index(axis)
    block = value.shape[0] // size
    nb = size.bit_length() - 1
    vals = {0: lax.dynamic_slice_in_dim(value, me * block, block, 0)}
    for o in range(1, size):
        wanted = lax.dynamic_slice_in_dim(value, (me ^ o) * block, block, 0)
        vals[o] = lax.ppermute(wanted, axis, [(i, i ^ o) for i in range(size)])
    return tree_sum(vals, nb)


def shift_cells(field, step):
    filler = jnp.zeros(field.shape[:-1] + (abs(step),), field.dtype)
    if step > 0:
        return jnp.concatenate([field[..., step:], filler], -1)
    return jnp.concatenate([filler, field[..., :step]], -1)


def local_dot(first, second):
    return jnp.sum(first * second, axis=(1, 2, 3))


def shards(macro_adjoint, slip_code, grain_id, grain_modulus, slip_softening, rve_spot):
    rve_count = slip_code.shape[0]
    cells = slip_code.shape[2]
    spot_count = macro_adjoint.shape[0] * lax.axis_size("hot")
    column = jnp.arange(cells) % RES
    upper_mask = (column != RES - 1).astype(jnp.float32)
    lower_mask = (column != 0).astype(jnp.float32)
    table = jnp.concatenate([grain_modulus[None, :], slip_softening.T], 0)

    def stiff_one(inputs):
        codes, grain_cells = inputs
        flat_codes = codes.reshape(-1)
        flat_grains = grain_cells.reshape(-1)
        onehot = (jnp.arange(GRAINS)[:, None] == flat_grains[None, :]).astype(jnp.float32)
        looked = jnp.dot(
            table, onehot, precision=lax.Precision.HIGHEST, preferred_element_type=jnp.float32
        )
        softening = jnp.zeros(flat_codes.shape, jnp.float32)
        for slip in range(SLIPS):
            active = (flat_codes // 2**slip % 2).astype(jnp.float32)
            softening = softening + active * looked[1 + slip]
        return (looked[0] / (1.0 + softening)).reshape(codes.shape)

    spot_onehot = (rve_spot[:, None] == jnp.arange(spot_count)[None, :]).astype(jnp.float32)
    parts, hot_me = axis_gather(macro_adjoint, "hot")
    if hot_me is None:
        all_strains = parts[0]
    else:
        local = macro_adjoint.shape[0]
        ordered = []
        for j in range(len(parts)):
            pick = [(hot_me ^ o) == j for o in range(len(parts))]
            block = parts[0]
            for o in range(1, len(parts)):
                block = jnp.where(pick[o], parts[o], block)
            ordered.append(block)
        all_strains = jnp.concatenate(ordered, 0)
    strains = jnp.dot(
        spot_onehot,
        all_strains,
        precision=lax.Precision.HIGHEST,
        preferred_element_type=jnp.float32,
    )
    stiff_slabs = stiff_one((slip_code, grain_id))
    stiff = lax.all_to_all(stiff_slabs, "xc", 0, 1, tiled=True)
    mine = lax.axis_index("xc")
    strains = lax.dynamic_slice_in_dim(strains, mine, 1, 0)
    padded = padded_2(stiff, (("yb", 1),), 1)

    def squares(residual):
        return axis_sum(local_dot(residual, residual), "yb")

    near_xup = padded[:, 2:]
    near_xdn = padded[:, :-2]
    near_yup = shift_cells(stiff, RES)
    near_ydn = shift_cells(stiff, -RES)
    near_zup = shift_cells(stiff, 1) * upper_mask
    near_zdn = shift_cells(stiff, -1) * lower_mask
    face_xup = 0.5 * (stiff + near_xup)
    face_xdn = 0.5 * (stiff + near_xdn)
    face_yup = 0.5 * (stiff + near_yup)
    face_ydn = 0.5 * (stiff + near_ydn)
    face_zup = 0.5 * (stiff + near_zup)
    face_zdn = 0.5 * (stiff + near_zdn)
    diagonal_sum = (mass_term + face_xup + face_xdn + face_yup + face_ydn + face_zup + face_zdn)[
        :, None
    ]
    gradients = [
        0.5 * (near_xup - near_xdn),
        0.5 * (near_yup - near_ydn),
        0.5 * (near_zup - near_zdn),
    ]
    tensor = [
        [strains[:, 0], strains[:, 5], strains[:, 4]],
        [strains[:, 5], strains[:, 1], strains[:, 3]],
        [strains[:, 4], strains[:, 3], strains[:, 2]],
    ]
    source = jnp.stack(
        [
            gradients[0] * tensor[comp][0][:, None, None]
            + gradients[1] * tensor[comp][1][:, None, None]
            + gradients[2] * tensor[comp][2][:, None, None]
            for comp in range(3)
        ],
        1,
    )

    def expand(values):
        return values[:, None, None, None]

    answer = jnp.zeros_like(source)
    residual = source
    direction = source
    norm_now = squares(residual)
    wide = padded_2(direction, (("yb", 2),), 1)
    for step in range(ITERS):
        image = (
            diagonal_sum * direction
            - face_xup[:, None] * wide[:, :, 2:]
            - face_xdn[:, None] * wide[:, :, :-2]
            - face_yup[:, None] * shift_cells(direction, RES)
            - face_ydn[:, None] * shift_cells(direction, -RES)
            - face_zup[:, None] * (shift_cells(direction, 1) * upper_mask)
            - face_zdn[:, None] * (shift_cells(direction, -1) * lower_mask)
        )
        alpha = norm_now / axis_sum(local_dot(direction, image), "yb")
        answer = answer + expand(alpha) * direction
        residual = residual - expand(alpha) * image
        norm_next = squares(residual)
        beta = expand(norm_next / norm_now)
        if step + 1 < ITERS:
            wide_residual = padded_2(residual, (("yb", 2),), 1)
            edges = jnp.concatenate([wide[:, :, :1], wide[:, :, -1:]], 2)
            edges_residual = jnp.concatenate([wide_residual[:, :, :1], wide_residual[:, :, -1:]], 2)
            edges = edges_residual + beta * edges
        direction = residual + beta * direction
        if step + 1 < ITERS:
            wide = jnp.concatenate([edges[:, :, :1], direction, edges[:, :, 1:]], 2)
        norm_now = norm_next
    volume = float(RES**3)
    stiff_part = jnp.sum(stiff, axis=(1, 2)) / volume
    moment = [
        [jnp.sum(answer[:, comp] * gradients[other], axis=(1, 2)) for other in range(3)]
        for comp in range(3)
    ]
    pairs = [(0, 0), (1, 1), (2, 2), (1, 2), (0, 2), (0, 1)]
    partial_here = jnp.stack(
        [
            stiff_part * strains[:, slot]
            - 0.5
            * (moment[pairs[slot][0]][pairs[slot][1]] + moment[pairs[slot][1]][pairs[slot][0]])
            / volume
            for slot in range(6)
        ],
        1,
    )
    per_spot = float(rve_count * lax.axis_size("hot") // spot_count)
    rve_one = axis_sum(partial_here, "yb")
    placed = (jnp.arange(rve_count)[:, None] == mine).astype(jnp.float32) * rve_one
    rve_totals = axis_sum(placed, "xc")
    spot_local = jnp.dot(
        spot_onehot.T,
        rve_totals,
        precision=lax.Precision.HIGHEST,
        preferred_element_type=jnp.float32,
    )
    owned = axis_reduce_scatter(spot_local, "hot")
    return (owned / per_spot, lax.all_to_all(answer, "xc", 2, 0, tiled=True))


def solution(mesh):
    hot, dom = mesh.shape["hot"], mesh.shape["dom"]
    rves_here = RVES // hot
    grouped = Mesh(mesh.devices.reshape(hot, dom // rves_here, rves_here), ("hot", "yb", "xc"))
    return jax.shard_map(
        shards,
        mesh=grouped,
        in_specs=(
            P("hot", None),
            P("hot", ("yb", "xc"), None),
            P("hot", ("yb", "xc"), None),
            P(),
            P(),
            P("hot"),
        ),
        out_specs=(P("hot", None), P("hot", None, ("yb", "xc"), None)),
        check_vma=False,
    )
```

```python
import jax
import jax.numpy as jnp
from jax import lax
from jax.sharding import Mesh, PartitionSpec as P

RES = 64
SLIPS = 12
GRAINS = 64
ITERS = 8
RVES = 32


mass_term = 0.02


def padded_2(value, sides, width):
    for axis, dim in sides:
        devices, length = (lax.axis_size(axis), value.shape[dim])
        up = [(i, (i + 1) % devices) for i in range(devices - 1)]
        down = [(j, i) for i, j in up]
        last = lax.slice_in_dim(value, length - width, length, axis=dim)
        leading = lax.slice_in_dim(value, 0, width, axis=dim)
        before = lax.ppermute(last, axis, up)
        after = lax.ppermute(leading, axis, down)
        value = jnp.concatenate([before, value, after], axis=dim)
    return value


def xor_groups(size):
    bits = size.bit_length() - 1
    if size != 1 << bits:
        return None
    groups = [(0, 1)] if bits % 2 else []
    lo = bits % 2
    while lo < bits:
        groups.append((lo, 2))
        lo += 2
    return groups


def tree_sum(vals, nb):
    cur = dict(vals)
    for level in range(nb):
        cur = {o: v + cur[o | (1 << level)] for o, v in cur.items() if not o & (1 << level)}
    return cur[0]


def axis_sum(value, axis):
    size = lax.axis_size(axis)
    groups = xor_groups(size)
    if groups is None:
        return lax.psum(value, axis)
    for lo, nb in groups:
        vals = {0: value}
        for o in range(1, 1 << nb):
            mask = o << lo
            vals[o] = lax.ppermute(value, axis, [(i, i ^ mask) for i in range(size)])
        value = tree_sum(vals, nb)
    return value


def axis_gather(value, axis):
    size = lax.axis_size(axis)
    if xor_groups(size) is None:
        return [lax.all_gather(value, axis, axis=0, tiled=True)], None
    parts = [value] + [
        lax.ppermute(value, axis, [(i, i ^ o) for i in range(size)]) for o in range(1, size)
    ]
    return parts, lax.axis_index(axis)


def axis_reduce_scatter(value, axis):
    size = lax.axis_size(axis)
    if xor_groups(size) is None:
        return lax.psum_scatter(value, axis, scatter_dimension=0, tiled=True)
    me = lax.axis_index(axis)
    block = value.shape[0] // size
    nb = size.bit_length() - 1
    vals = {0: lax.dynamic_slice_in_dim(value, me * block, block, 0)}
    for o in range(1, size):
        wanted = lax.dynamic_slice_in_dim(value, (me ^ o) * block, block, 0)
        vals[o] = lax.ppermute(wanted, axis, [(i, i ^ o) for i in range(size)])
    return tree_sum(vals, nb)


def shift_cells(field, step):
    filler = jnp.zeros(field.shape[:-1] + (abs(step),), field.dtype)
    if step > 0:
        return jnp.concatenate([field[..., step:], filler], -1)
    return jnp.concatenate([filler, field[..., :step]], -1)


def local_dot(first, second):
    return jnp.sum(first * second, axis=(1, 2, 3))


def shards(macro_adjoint, slip_code, grain_id, grain_modulus, slip_softening, rve_spot):
    rve_count = slip_code.shape[0]
    cells = slip_code.shape[2]
    spot_count = macro_adjoint.shape[0] * lax.axis_size("hot")
    column = jnp.arange(cells) % RES
    upper_mask = (column != RES - 1).astype(jnp.float32)
    lower_mask = (column != 0).astype(jnp.float32)
    table = jnp.concatenate([grain_modulus[None, :], slip_softening.T], 0)

    def stiff_one(inputs):
        codes, grain_cells = inputs
        flat_codes = codes.reshape(-1)
        flat_grains = grain_cells.reshape(-1)
        onehot = (jnp.arange(GRAINS)[:, None] == flat_grains[None, :]).astype(jnp.float32)
        looked = jnp.dot(
            table, onehot, precision=lax.Precision.HIGHEST, preferred_element_type=jnp.float32
        )
        softening = jnp.zeros(flat_codes.shape, jnp.float32)
        for slip in range(SLIPS):
            active = (flat_codes // 2**slip % 2).astype(jnp.float32)
            softening = softening + active * looked[1 + slip]
        return (looked[0] / (1.0 + softening)).reshape(codes.shape)

    spot_onehot = (rve_spot[:, None] == jnp.arange(spot_count)[None, :]).astype(jnp.float32)
    parts, hot_me = axis_gather(macro_adjoint, "hot")
    if hot_me is None:
        all_strains = parts[0]
    else:
        local = macro_adjoint.shape[0]
        ordered = []
        for j in range(len(parts)):
            pick = [(hot_me ^ o) == j for o in range(len(parts))]
            block = parts[0]
            for o in range(1, len(parts)):
                block = jnp.where(pick[o], parts[o], block)
            ordered.append(block)
        all_strains = jnp.concatenate(ordered, 0)
    strains = jnp.dot(
        spot_onehot,
        all_strains,
        precision=lax.Precision.HIGHEST,
        preferred_element_type=jnp.float32,
    )
    stiff_slabs = stiff_one((slip_code, grain_id))
    stiff = lax.all_to_all(stiff_slabs, "xc", 0, 1, tiled=True)
    mine = lax.axis_index("xc")
    strains = lax.dynamic_slice_in_dim(strains, mine, 1, 0)
    padded = padded_2(stiff, (("yb", 1),), 1)

    def squares(residual):
        return axis_sum(local_dot(residual, residual), "yb")

    near_xup = padded[:, 2:]
    near_xdn = padded[:, :-2]
    near_yup = shift_cells(stiff, RES)
    near_ydn = shift_cells(stiff, -RES)
    near_zup = shift_cells(stiff, 1) * upper_mask
    near_zdn = shift_cells(stiff, -1) * lower_mask
    face_xup = 0.5 * (stiff + near_xup)
    face_xdn = 0.5 * (stiff + near_xdn)
    face_yup = 0.5 * (stiff + near_yup)
    face_ydn = 0.5 * (stiff + near_ydn)
    face_zup = 0.5 * (stiff + near_zup)
    face_zdn = 0.5 * (stiff + near_zdn)
    diagonal_sum = (mass_term + face_xup + face_xdn + face_yup + face_ydn + face_zup + face_zdn)[
        :, None
    ]
    gradients = [
        0.5 * (near_xup - near_xdn),
        0.5 * (near_yup - near_ydn),
        0.5 * (near_zup - near_zdn),
    ]
    tensor = [
        [strains[:, 0], strains[:, 5], strains[:, 4]],
        [strains[:, 5], strains[:, 1], strains[:, 3]],
        [strains[:, 4], strains[:, 3], strains[:, 2]],
    ]
    source = jnp.stack(
        [
            gradients[0] * tensor[comp][0][:, None, None]
            + gradients[1] * tensor[comp][1][:, None, None]
            + gradients[2] * tensor[comp][2][:, None, None]
            for comp in range(3)
        ],
        1,
    )

    def expand(values):
        return values[:, None, None, None]

    def boundary_planes(value):
        size = lax.axis_size("yb")
        up = [(i, i + 1) for i in range(size - 1)]
        down = [(i + 1, i) for i in range(size - 1)]
        before = lax.ppermute(value[:, :, -1:], "yb", up)
        after = lax.ppermute(value[:, :, :1], "yb", down)
        return jnp.concatenate([before, after], 2)

    def operate(direction, edges):
        wide = jnp.concatenate([edges[:, :, :1], direction, edges[:, :, 1:]], 2)
        return (
            diagonal_sum * direction
            - face_xup[:, None] * wide[:, :, 2:]
            - face_xdn[:, None] * wide[:, :, :-2]
            - face_yup[:, None] * shift_cells(direction, RES)
            - face_ydn[:, None] * shift_cells(direction, -RES)
            - face_zup[:, None] * (shift_cells(direction, 1) * upper_mask)
            - face_zdn[:, None] * (shift_cells(direction, -1) * lower_mask)
        )

    answer = jnp.zeros_like(source)
    residual = source
    direction = source
    residual_edges = boundary_planes(source)
    direction_edges = residual_edges
    for step in range(ITERS):
        image = operate(direction, direction_edges)
        last = step + 1 == ITERS
        if not last:
            image_edges = boundary_planes(image)
        local = jnp.stack(
            [
                local_dot(direction, image),
                local_dot(residual, residual),
                local_dot(residual, image),
                local_dot(image, image),
            ],
            -1,
        )
        sums = axis_sum(local, "yb")
        norm_now = sums[:, 1]
        alpha = norm_now / sums[:, 0]
        answer = answer + expand(alpha) * direction
        if last:
            break
        norm_next = norm_now - 2.0 * alpha * sums[:, 2] + alpha * alpha * sums[:, 3]
        beta = expand(norm_next / norm_now)
        residual = residual - expand(alpha) * image
        residual_edges = residual_edges - expand(alpha) * image_edges
        direction = residual + beta * direction
        direction_edges = residual_edges + beta * direction_edges
    volume = float(RES**3)
    stiff_part = jnp.sum(stiff, axis=(1, 2)) / volume
    moment = [
        [jnp.sum(answer[:, comp] * gradients[other], axis=(1, 2)) for other in range(3)]
        for comp in range(3)
    ]
    pairs = [(0, 0), (1, 1), (2, 2), (1, 2), (0, 2), (0, 1)]
    partial_here = jnp.stack(
        [
            stiff_part * strains[:, slot]
            - 0.5
            * (moment[pairs[slot][0]][pairs[slot][1]] + moment[pairs[slot][1]][pairs[slot][0]])
            / volume
            for slot in range(6)
        ],
        1,
    )
    per_spot = float(rve_count * lax.axis_size("hot") // spot_count)
    rve_one = axis_sum(partial_here, "yb")
    placed = (jnp.arange(rve_count)[:, None] == mine).astype(jnp.float32) * rve_one
    rve_totals = axis_sum(placed, "xc")
    spot_local = jnp.dot(
        spot_onehot.T,
        rve_totals,
        precision=lax.Precision.HIGHEST,
        preferred_element_type=jnp.float32,
    )
    owned = axis_reduce_scatter(spot_local, "hot")
    return (owned / per_spot, lax.all_to_all(answer, "xc", 2, 0, tiled=True))


def solution(mesh):
    hot, dom = mesh.shape["hot"], mesh.shape["dom"]
    rves_here = RVES // hot
    grouped = Mesh(mesh.devices.reshape(hot, dom // rves_here, rves_here), ("hot", "yb", "xc"))
    return jax.shard_map(
        shards,
        mesh=grouped,
        in_specs=(
            P("hot", None),
            P("hot", ("yb", "xc"), None),
            P("hot", ("yb", "xc"), None),
            P(),
            P(),
            P("hot"),
        ),
        out_specs=(P("hot", None), P("hot", None, ("yb", "xc"), None)),
        check_vma=False,
    )
```

```python
import jax
import jax.numpy as jnp
from jax import lax
from jax.sharding import Mesh, PartitionSpec as P

RES = 64
SLIPS = 12
GRAINS = 64
ITERS = 8
RVES = 32


mass_term = 0.02


def padded_2(value, sides, width):
    for axis, dim in sides:
        devices, length = (lax.axis_size(axis), value.shape[dim])
        up = [(i, (i + 1) % devices) for i in range(devices - 1)]
        down = [(j, i) for i, j in up]
        last = lax.slice_in_dim(value, length - width, length, axis=dim)
        leading = lax.slice_in_dim(value, 0, width, axis=dim)
        before = lax.ppermute(last, axis, up)
        after = lax.ppermute(leading, axis, down)
        value = jnp.concatenate([before, value, after], axis=dim)
    return value


def xor_groups(size):
    bits = size.bit_length() - 1
    if size != 1 << bits:
        return None
    groups = [(0, 1)] if bits % 2 else []
    lo = bits % 2
    while lo < bits:
        groups.append((lo, 2))
        lo += 2
    return groups


def tree_sum(vals, nb):
    cur = dict(vals)
    for level in range(nb):
        cur = {o: v + cur[o | (1 << level)] for o, v in cur.items() if not o & (1 << level)}
    return cur[0]


def axis_sum(value, axis):
    size = lax.axis_size(axis)
    groups = xor_groups(size)
    if groups is None:
        return lax.psum(value, axis)
    for lo, nb in groups:
        vals = {0: value}
        for o in range(1, 1 << nb):
            mask = o << lo
            vals[o] = lax.ppermute(value, axis, [(i, i ^ mask) for i in range(size)])
        value = tree_sum(vals, nb)
    return value


def axis_gather(value, axis):
    size = lax.axis_size(axis)
    if xor_groups(size) is None:
        return [lax.all_gather(value, axis, axis=0, tiled=True)], None
    parts = [value] + [
        lax.ppermute(value, axis, [(i, i ^ o) for i in range(size)]) for o in range(1, size)
    ]
    return parts, lax.axis_index(axis)


def axis_reduce_scatter(value, axis):
    size = lax.axis_size(axis)
    if xor_groups(size) is None:
        return lax.psum_scatter(value, axis, scatter_dimension=0, tiled=True)
    me = lax.axis_index(axis)
    block = value.shape[0] // size
    nb = size.bit_length() - 1
    vals = {0: lax.dynamic_slice_in_dim(value, me * block, block, 0)}
    for o in range(1, size):
        wanted = lax.dynamic_slice_in_dim(value, (me ^ o) * block, block, 0)
        vals[o] = lax.ppermute(wanted, axis, [(i, i ^ o) for i in range(size)])
    return tree_sum(vals, nb)


def shift_cells(field, step):
    filler = jnp.zeros(field.shape[:-1] + (abs(step),), field.dtype)
    if step > 0:
        return jnp.concatenate([field[..., step:], filler], -1)
    return jnp.concatenate([filler, field[..., :step]], -1)


def local_dot(first, second):
    return jnp.sum(first * second, axis=(1, 2, 3))


def shards(macro_adjoint, slip_code, grain_id, grain_modulus, slip_softening, rve_spot):
    rve_count = slip_code.shape[0]
    cells = slip_code.shape[2]
    spot_count = macro_adjoint.shape[0] * lax.axis_size("hot")
    column = jnp.arange(cells) % RES
    upper_mask = (column != RES - 1).astype(jnp.float32)
    lower_mask = (column != 0).astype(jnp.float32)
    table = jnp.concatenate([grain_modulus[None, :], slip_softening.T], 0)

    def stiff_one(inputs):
        codes, grain_cells = inputs
        flat_codes = codes.reshape(-1)
        flat_grains = grain_cells.reshape(-1)
        onehot = (jnp.arange(GRAINS)[:, None] == flat_grains[None, :]).astype(jnp.float32)
        looked = jnp.dot(
            table, onehot, precision=lax.Precision.HIGHEST, preferred_element_type=jnp.float32
        )
        softening = jnp.zeros(flat_codes.shape, jnp.float32)
        for slip in range(SLIPS):
            active = (flat_codes // 2**slip % 2).astype(jnp.float32)
            softening = softening + active * looked[1 + slip]
        return (looked[0] / (1.0 + softening)).reshape(codes.shape)

    spot_onehot = (rve_spot[:, None] == jnp.arange(spot_count)[None, :]).astype(jnp.float32)
    parts, hot_me = axis_gather(macro_adjoint, "hot")
    if hot_me is None:
        all_strains = parts[0]
    else:
        local = macro_adjoint.shape[0]
        ordered = []
        for j in range(len(parts)):
            pick = [(hot_me ^ o) == j for o in range(len(parts))]
            block = parts[0]
            for o in range(1, len(parts)):
                block = jnp.where(pick[o], parts[o], block)
            ordered.append(block)
        all_strains = jnp.concatenate(ordered, 0)
    strains = jnp.dot(
        spot_onehot,
        all_strains,
        precision=lax.Precision.HIGHEST,
        preferred_element_type=jnp.float32,
    )
    stiff_slabs = stiff_one((slip_code, grain_id))
    stiff = lax.all_to_all(stiff_slabs, "xc", 0, 1, tiled=True)
    mine = lax.axis_index("xc")
    strains = lax.dynamic_slice_in_dim(strains, mine, 1, 0)
    padded = padded_2(stiff, (("yb", 1),), 1)

    def squares(residual):
        return axis_sum(local_dot(residual, residual), "yb")

    near_xup = padded[:, 2:]
    near_xdn = padded[:, :-2]
    near_yup = shift_cells(stiff, RES)
    near_ydn = shift_cells(stiff, -RES)
    near_zup = shift_cells(stiff, 1) * upper_mask
    near_zdn = shift_cells(stiff, -1) * lower_mask
    face_xup = 0.5 * (stiff + near_xup)
    face_xdn = 0.5 * (stiff + near_xdn)
    face_yup = 0.5 * (stiff + near_yup)
    face_ydn = 0.5 * (stiff + near_ydn)
    face_zup = 0.5 * (stiff + near_zup)
    face_zdn = 0.5 * (stiff + near_zdn)
    diagonal_sum = (mass_term + face_xup + face_xdn + face_yup + face_ydn + face_zup + face_zdn)[
        :, None
    ]
    gradients = [
        0.5 * (near_xup - near_xdn),
        0.5 * (near_yup - near_ydn),
        0.5 * (near_zup - near_zdn),
    ]
    tensor = [
        [strains[:, 0], strains[:, 5], strains[:, 4]],
        [strains[:, 5], strains[:, 1], strains[:, 3]],
        [strains[:, 4], strains[:, 3], strains[:, 2]],
    ]
    source = jnp.stack(
        [
            gradients[0] * tensor[comp][0][:, None, None]
            + gradients[1] * tensor[comp][1][:, None, None]
            + gradients[2] * tensor[comp][2][:, None, None]
            for comp in range(3)
        ],
        1,
    )

    def expand(values):
        return values[:, None, None, None]

    def boundary_planes(value):
        size = lax.axis_size("yb")
        up = [(i, i + 1) for i in range(size - 1)]
        down = [(i + 1, i) for i in range(size - 1)]
        before = lax.ppermute(value[:, :, -1:], "yb", up)
        after = lax.ppermute(value[:, :, :1], "yb", down)
        return jnp.concatenate([before, after], 2)

    def operate(direction, edges):
        wide = jnp.concatenate([edges[:, :, :1], direction, edges[:, :, 1:]], 2)
        return (
            diagonal_sum * direction
            - face_xup[:, None] * wide[:, :, 2:]
            - face_xdn[:, None] * wide[:, :, :-2]
            - face_yup[:, None] * shift_cells(direction, RES)
            - face_ydn[:, None] * shift_cells(direction, -RES)
            - face_zup[:, None] * (shift_cells(direction, 1) * upper_mask)
            - face_zdn[:, None] * (shift_cells(direction, -1) * lower_mask)
        )

    answer = jnp.zeros_like(source)
    residual = source
    direction = source
    residual_edges = boundary_planes(source)
    direction_edges = residual_edges
    for step in range(ITERS):
        image = operate(direction, direction_edges)
        last = step + 1 == ITERS
        if not last:
            image_edges = boundary_planes(image)
        local = jnp.stack(
            [
                local_dot(direction, image),
                local_dot(residual, residual),
                local_dot(residual, image),
                local_dot(image, image),
            ],
            -1,
        )
        sums = jnp.broadcast_to(axis_sum(local, "yb")[:, None, None, :], (1, 1, 8, 4))
        norm_now = sums[..., 1:2]
        alpha = norm_now / sums[..., 0:1]
        answer = answer + alpha[:, :, :1] * direction
        if last:
            break
        norm_next = norm_now - 2.0 * alpha * sums[..., 2:3] + alpha * alpha * sums[..., 3:4]
        beta = (norm_next / norm_now)[:, :, :1]
        alpha = alpha[:, :, :1]
        residual = residual - alpha * image
        residual_edges = residual_edges - alpha * image_edges
        direction = residual + beta * direction
        direction_edges = residual_edges + beta * direction_edges
    volume = float(RES**3)
    stiff_part = jnp.sum(stiff, axis=(1, 2)) / volume
    moment = [
        [jnp.sum(answer[:, comp] * gradients[other], axis=(1, 2)) for other in range(3)]
        for comp in range(3)
    ]
    pairs = [(0, 0), (1, 1), (2, 2), (1, 2), (0, 2), (0, 1)]
    partial_here = jnp.stack(
        [
            stiff_part * strains[:, slot]
            - 0.5
            * (moment[pairs[slot][0]][pairs[slot][1]] + moment[pairs[slot][1]][pairs[slot][0]])
            / volume
            for slot in range(6)
        ],
        1,
    )
    per_spot = float(rve_count * lax.axis_size("hot") // spot_count)
    rve_one = axis_sum(partial_here, "yb")
    placed = (jnp.arange(rve_count)[:, None] == mine).astype(jnp.float32) * rve_one
    rve_totals = axis_sum(placed, "xc")
    spot_local = jnp.dot(
        spot_onehot.T,
        rve_totals,
        precision=lax.Precision.HIGHEST,
        preferred_element_type=jnp.float32,
    )
    owned = axis_reduce_scatter(spot_local, "hot")
    return (owned / per_spot, lax.all_to_all(answer, "xc", 2, 0, tiled=True))


def solution(mesh):
    hot, dom = mesh.shape["hot"], mesh.shape["dom"]
    rves_here = RVES // hot
    grouped = Mesh(mesh.devices.reshape(hot, dom // rves_here, rves_here), ("hot", "yb", "xc"))
    return jax.shard_map(
        shards,
        mesh=grouped,
        in_specs=(
            P("hot", None),
            P("hot", ("yb", "xc"), None),
            P("hot", ("yb", "xc"), None),
            P(),
            P(),
            P("hot"),
        ),
        out_specs=(P("hot", None), P("hot", None, ("yb", "xc"), None)),
        check_vma=False,
    )
```

```python
import jax
import jax.numpy as jnp
from jax import lax
from jax.experimental import pallas as pl
from jax.sharding import Mesh, PartitionSpec as P

RES = 64
SLIPS = 12
GRAINS = 64
ITERS = 8
RVES = 32


mass_term = 0.02


def padded_2(value, sides, width):
    for axis, dim in sides:
        devices, length = (lax.axis_size(axis), value.shape[dim])
        up = [(i, (i + 1) % devices) for i in range(devices - 1)]
        down = [(j, i) for i, j in up]
        last = lax.slice_in_dim(value, length - width, length, axis=dim)
        leading = lax.slice_in_dim(value, 0, width, axis=dim)
        before = lax.ppermute(last, axis, up)
        after = lax.ppermute(leading, axis, down)
        value = jnp.concatenate([before, value, after], axis=dim)
    return value


def xor_groups(size):
    bits = size.bit_length() - 1
    if size != 1 << bits:
        return None
    groups = [(0, 1)] if bits % 2 else []
    lo = bits % 2
    while lo < bits:
        groups.append((lo, 2))
        lo += 2
    return groups


def tree_sum(vals, nb):
    cur = dict(vals)
    for level in range(nb):
        cur = {o: v + cur[o | (1 << level)] for o, v in cur.items() if not o & (1 << level)}
    return cur[0]


def axis_sum(value, axis):
    size = lax.axis_size(axis)
    groups = xor_groups(size)
    if groups is None:
        return lax.psum(value, axis)
    for lo, nb in groups:
        vals = {0: value}
        for o in range(1, 1 << nb):
            mask = o << lo
            vals[o] = lax.ppermute(value, axis, [(i, i ^ mask) for i in range(size)])
        value = tree_sum(vals, nb)
    return value


def axis_gather(value, axis):
    size = lax.axis_size(axis)
    if xor_groups(size) is None:
        return [lax.all_gather(value, axis, axis=0, tiled=True)], None
    parts = [value] + [
        lax.ppermute(value, axis, [(i, i ^ o) for i in range(size)]) for o in range(1, size)
    ]
    return parts, lax.axis_index(axis)


def axis_reduce_scatter(value, axis):
    size = lax.axis_size(axis)
    if xor_groups(size) is None:
        return lax.psum_scatter(value, axis, scatter_dimension=0, tiled=True)
    me = lax.axis_index(axis)
    block = value.shape[0] // size
    nb = size.bit_length() - 1
    vals = {0: lax.dynamic_slice_in_dim(value, me * block, block, 0)}
    for o in range(1, size):
        wanted = lax.dynamic_slice_in_dim(value, (me ^ o) * block, block, 0)
        vals[o] = lax.ppermute(wanted, axis, [(i, i ^ o) for i in range(size)])
    return tree_sum(vals, nb)


CHUNK = 512


def stiffness_kernel(pieces_ref, codes_ref, grains_ref, out_ref):
    rows = pieces_ref.shape[1]

    def chunk(c, carry):
        at = pl.multiple_of(c * CHUNK, CHUNK)
        for plane in range(codes_ref.shape[1]):
            grains = grains_ref[0, plane : plane + 1, pl.ds(at, CHUNK)]
            codes = codes_ref[0, plane : plane + 1, pl.ds(at, CHUNK)]
            onehot = (lax.broadcasted_iota(jnp.int32, (GRAINS, CHUNK), 0) == grains).astype(jnp.bfloat16)
            looked = jnp.dot(pieces_ref[0], onehot, preferred_element_type=jnp.float32)
            looked = looked + jnp.dot(pieces_ref[1], onehot, preferred_element_type=jnp.float32)
            looked = looked + jnp.dot(pieces_ref[2], onehot, preferred_element_type=jnp.float32)
            softening = jnp.zeros((1, CHUNK), jnp.float32)
            for slip in range(SLIPS):
                active = ((codes >> slip) & 1).astype(jnp.float32)
                softening = softening + active * looked[1 + slip : 2 + slip, :]
            out_ref[0, plane : plane + 1, pl.ds(at, CHUNK)] = looked[0:1, :] / (1.0 + softening)
        return carry

    lax.fori_loop(0, codes_ref.shape[2] // CHUNK, chunk, 0)
    del rows


def stiffness(table, slip_code, grain_id):
    high = lax.reduce_precision(table, exponent_bits=8, mantissa_bits=7)
    rest = table - high
    middle = lax.reduce_precision(rest, exponent_bits=8, mantissa_bits=7)
    low = rest - middle
    pieces = jnp.stack([high, middle, low]).astype(jnp.bfloat16)
    pieces = jnp.pad(pieces, ((0, 0), (0, 16 - table.shape[0]), (0, 0)))
    rves, planes, cells = slip_code.shape
    block = pl.BlockSpec((1, planes, cells), lambda r: (r, 0, 0))
    return pl.pallas_call(
        stiffness_kernel,
        grid=(rves,),
        in_specs=[pl.BlockSpec(pieces.shape, lambda r: (0, 0, 0)), block, block],
        out_specs=block,
        out_shape=jax.ShapeDtypeStruct(slip_code.shape, jnp.float32),
    )(pieces, slip_code, grain_id)


def shift_cells(field, step):
    filler = jnp.zeros(field.shape[:-1] + (abs(step),), field.dtype)
    if step > 0:
        return jnp.concatenate([field[..., step:], filler], -1)
    return jnp.concatenate([filler, field[..., :step]], -1)


def local_dot(first, second):
    return jnp.sum(first * second, axis=(1, 2, 3))


def shards(macro_adjoint, slip_code, grain_id, grain_modulus, slip_softening, rve_spot):
    rve_count = slip_code.shape[0]
    cells = slip_code.shape[2]
    spot_count = macro_adjoint.shape[0] * lax.axis_size("hot")
    column = jnp.arange(cells) % RES
    upper_mask = (column != RES - 1).astype(jnp.float32)
    lower_mask = (column != 0).astype(jnp.float32)
    table = jnp.concatenate([grain_modulus[None, :], slip_softening.T], 0)

    def stiff_one(inputs):
        codes, grain_cells = inputs
        flat_codes = codes.reshape(-1)
        flat_grains = grain_cells.reshape(-1)
        onehot = (jnp.arange(GRAINS)[:, None] == flat_grains[None, :]).astype(jnp.float32)
        looked = jnp.dot(
            table, onehot, precision=lax.Precision.HIGHEST, preferred_element_type=jnp.float32
        )
        softening = jnp.zeros(flat_codes.shape, jnp.float32)
        for slip in range(SLIPS):
            active = (flat_codes // 2**slip % 2).astype(jnp.float32)
            softening = softening + active * looked[1 + slip]
        return (looked[0] / (1.0 + softening)).reshape(codes.shape)

    spot_onehot = (rve_spot[:, None] == jnp.arange(spot_count)[None, :]).astype(jnp.float32)
    parts, hot_me = axis_gather(macro_adjoint, "hot")
    if hot_me is None:
        all_strains = parts[0]
    else:
        local = macro_adjoint.shape[0]
        ordered = []
        for j in range(len(parts)):
            pick = [(hot_me ^ o) == j for o in range(len(parts))]
            block = parts[0]
            for o in range(1, len(parts)):
                block = jnp.where(pick[o], parts[o], block)
            ordered.append(block)
        all_strains = jnp.concatenate(ordered, 0)
    strains = jnp.dot(
        spot_onehot,
        all_strains,
        precision=lax.Precision.HIGHEST,
        preferred_element_type=jnp.float32,
    )
    stiff_slabs = stiffness(table, slip_code, grain_id)
    stiff = lax.all_to_all(stiff_slabs, "xc", 0, 1, tiled=True)
    mine = lax.axis_index("xc")
    strains = lax.dynamic_slice_in_dim(strains, mine, 1, 0)
    padded = padded_2(stiff, (("yb", 1),), 1)

    def squares(residual):
        return axis_sum(local_dot(residual, residual), "yb")

    near_xup = padded[:, 2:]
    near_xdn = padded[:, :-2]
    near_yup = shift_cells(stiff, RES)
    near_ydn = shift_cells(stiff, -RES)
    near_zup = shift_cells(stiff, 1) * upper_mask
    near_zdn = shift_cells(stiff, -1) * lower_mask
    face_xup = 0.5 * (stiff + near_xup)
    face_xdn = 0.5 * (stiff + near_xdn)
    face_yup = 0.5 * (stiff + near_yup)
    face_ydn = 0.5 * (stiff + near_ydn)
    face_zup = 0.5 * (stiff + near_zup)
    face_zdn = 0.5 * (stiff + near_zdn)
    diagonal_sum = (mass_term + face_xup + face_xdn + face_yup + face_ydn + face_zup + face_zdn)[
        :, None
    ]
    gradients = [
        0.5 * (near_xup - near_xdn),
        0.5 * (near_yup - near_ydn),
        0.5 * (near_zup - near_zdn),
    ]
    tensor = [
        [strains[:, 0], strains[:, 5], strains[:, 4]],
        [strains[:, 5], strains[:, 1], strains[:, 3]],
        [strains[:, 4], strains[:, 3], strains[:, 2]],
    ]
    source = jnp.stack(
        [
            gradients[0] * tensor[comp][0][:, None, None]
            + gradients[1] * tensor[comp][1][:, None, None]
            + gradients[2] * tensor[comp][2][:, None, None]
            for comp in range(3)
        ],
        1,
    )

    def expand(values):
        return values[:, None, None, None]

    def boundary_planes(value):
        size = lax.axis_size("yb")
        up = [(i, i + 1) for i in range(size - 1)]
        down = [(i + 1, i) for i in range(size - 1)]
        before = lax.ppermute(value[:, :, -1:], "yb", up)
        after = lax.ppermute(value[:, :, :1], "yb", down)
        return jnp.concatenate([before, after], 2)

    def operate(direction, edges):
        wide = jnp.concatenate([edges[:, :, :1], direction, edges[:, :, 1:]], 2)
        return (
            diagonal_sum * direction
            - face_xup[:, None] * wide[:, :, 2:]
            - face_xdn[:, None] * wide[:, :, :-2]
            - face_yup[:, None] * shift_cells(direction, RES)
            - face_ydn[:, None] * shift_cells(direction, -RES)
            - face_zup[:, None] * (shift_cells(direction, 1) * upper_mask)
            - face_zdn[:, None] * (shift_cells(direction, -1) * lower_mask)
        )

    answer = jnp.zeros_like(source)
    residual = source
    direction = source
    residual_edges = boundary_planes(source)
    direction_edges = residual_edges
    for step in range(ITERS):
        image = operate(direction, direction_edges)
        last = step + 1 == ITERS
        if not last:
            image_edges = boundary_planes(image)
        local = jnp.stack(
            [
                local_dot(direction, image),
                local_dot(residual, residual),
                local_dot(residual, image),
                local_dot(image, image),
            ],
            -1,
        )
        sums = axis_sum(local, "yb")
        norm_now = sums[:, 1]
        alpha = norm_now / sums[:, 0]
        answer = answer + expand(alpha) * direction
        if last:
            break
        norm_next = norm_now - 2.0 * alpha * sums[:, 2] + alpha * alpha * sums[:, 3]
        beta = expand(norm_next / norm_now)
        residual = residual - expand(alpha) * image
        residual_edges = residual_edges - expand(alpha) * image_edges
        direction = residual + beta * direction
        direction_edges = residual_edges + beta * direction_edges
    volume = float(RES**3)
    stiff_part = jnp.sum(stiff, axis=(1, 2)) / volume
    moment = [
        [jnp.sum(answer[:, comp] * gradients[other], axis=(1, 2)) for other in range(3)]
        for comp in range(3)
    ]
    pairs = [(0, 0), (1, 1), (2, 2), (1, 2), (0, 2), (0, 1)]
    partial_here = jnp.stack(
        [
            stiff_part * strains[:, slot]
            - 0.5
            * (moment[pairs[slot][0]][pairs[slot][1]] + moment[pairs[slot][1]][pairs[slot][0]])
            / volume
            for slot in range(6)
        ],
        1,
    )
    per_spot = float(rve_count * lax.axis_size("hot") // spot_count)
    rve_one = axis_sum(partial_here, "yb")
    placed = (jnp.arange(rve_count)[:, None] == mine).astype(jnp.float32) * rve_one
    rve_totals = axis_sum(placed, "xc")
    spot_local = jnp.dot(
        spot_onehot.T,
        rve_totals,
        precision=lax.Precision.HIGHEST,
        preferred_element_type=jnp.float32,
    )
    owned = axis_reduce_scatter(spot_local, "hot")
    return (owned / per_spot, lax.all_to_all(answer, "xc", 2, 0, tiled=True))


def solution(mesh):
    hot, dom = mesh.shape["hot"], mesh.shape["dom"]
    rves_here = RVES // hot
    grouped = Mesh(mesh.devices.reshape(hot, dom // rves_here, rves_here), ("hot", "yb", "xc"))
    return jax.shard_map(
        shards,
        mesh=grouped,
        in_specs=(
            P("hot", None),
            P("hot", ("yb", "xc"), None),
            P("hot", ("yb", "xc"), None),
            P(),
            P(),
            P("hot"),
        ),
        out_specs=(P("hot", None), P("hot", None, ("yb", "xc"), None)),
        check_vma=False,
    )
```

```python
import jax
import jax.numpy as jnp
from jax import lax
from jax.experimental import pallas as pl
from jax.sharding import Mesh, PartitionSpec as P

RES = 64
SLIPS = 12
GRAINS = 64
ITERS = 8
RVES = 32


mass_term = 0.02


def padded_2(value, sides, width):
    for axis, dim in sides:
        devices, length = (lax.axis_size(axis), value.shape[dim])
        up = [(i, (i + 1) % devices) for i in range(devices - 1)]
        down = [(j, i) for i, j in up]
        last = lax.slice_in_dim(value, length - width, length, axis=dim)
        leading = lax.slice_in_dim(value, 0, width, axis=dim)
        before = lax.ppermute(last, axis, up)
        after = lax.ppermute(leading, axis, down)
        value = jnp.concatenate([before, value, after], axis=dim)
    return value


def xor_groups(size):
    bits = size.bit_length() - 1
    if size != 1 << bits:
        return None
    groups = [(0, 1)] if bits % 2 else []
    lo = bits % 2
    while lo < bits:
        groups.append((lo, 2))
        lo += 2
    return groups


def tree_sum(vals, nb):
    cur = dict(vals)
    for level in range(nb):
        cur = {o: v + cur[o | (1 << level)] for o, v in cur.items() if not o & (1 << level)}
    return cur[0]


def axis_sum(value, axis):
    size = lax.axis_size(axis)
    groups = xor_groups(size)
    if groups is None:
        return lax.psum(value, axis)
    for lo, nb in groups:
        vals = {0: value}
        for o in range(1, 1 << nb):
            mask = o << lo
            vals[o] = lax.ppermute(value, axis, [(i, i ^ mask) for i in range(size)])
        value = tree_sum(vals, nb)
    return value


def axis_gather(value, axis):
    size = lax.axis_size(axis)
    if xor_groups(size) is None:
        return [lax.all_gather(value, axis, axis=0, tiled=True)], None
    parts = [value] + [
        lax.ppermute(value, axis, [(i, i ^ o) for i in range(size)]) for o in range(1, size)
    ]
    return parts, lax.axis_index(axis)


def axis_reduce_scatter(value, axis):
    size = lax.axis_size(axis)
    if xor_groups(size) is None:
        return lax.psum_scatter(value, axis, scatter_dimension=0, tiled=True)
    me = lax.axis_index(axis)
    block = value.shape[0] // size
    nb = size.bit_length() - 1
    vals = {0: lax.dynamic_slice_in_dim(value, me * block, block, 0)}
    for o in range(1, size):
        wanted = lax.dynamic_slice_in_dim(value, (me ^ o) * block, block, 0)
        vals[o] = lax.ppermute(wanted, axis, [(i, i ^ o) for i in range(size)])
    return tree_sum(vals, nb)


CHUNK = 512


def stiffness_kernel(pieces_ref, codes_ref, grains_ref, out_ref):
    rows = pieces_ref.shape[1]

    def chunk(c, carry):
        at = pl.multiple_of(c * CHUNK, CHUNK)
        for plane in range(codes_ref.shape[1]):
            grains = grains_ref[0, plane : plane + 1, pl.ds(at, CHUNK)]
            codes = codes_ref[0, plane : plane + 1, pl.ds(at, CHUNK)]
            onehot = (lax.broadcasted_iota(jnp.int32, (GRAINS, CHUNK), 0) == grains).astype(jnp.bfloat16)
            looked = jnp.dot(pieces_ref[0], onehot, preferred_element_type=jnp.float32)
            looked = looked + jnp.dot(pieces_ref[1], onehot, preferred_element_type=jnp.float32)
            looked = looked + jnp.dot(pieces_ref[2], onehot, preferred_element_type=jnp.float32)
            softening = jnp.zeros((1, CHUNK), jnp.float32)
            for slip in range(SLIPS):
                active = ((codes >> slip) & 1).astype(jnp.float32)
                softening = softening + active * looked[1 + slip : 2 + slip, :]
            out_ref[0, plane : plane + 1, pl.ds(at, CHUNK)] = looked[0:1, :] / (1.0 + softening)
        return carry

    lax.fori_loop(0, codes_ref.shape[2] // CHUNK, chunk, 0)
    del rows


def stiffness(table, slip_code, grain_id):
    high = lax.reduce_precision(table, exponent_bits=8, mantissa_bits=7)
    rest = table - high
    middle = lax.reduce_precision(rest, exponent_bits=8, mantissa_bits=7)
    low = rest - middle
    pieces = jnp.stack([high, middle, low]).astype(jnp.bfloat16)
    pieces = jnp.pad(pieces, ((0, 0), (0, 16 - table.shape[0]), (0, 0)))
    rves, planes, cells = slip_code.shape
    block = pl.BlockSpec((1, planes, cells), lambda r: (r, 0, 0))
    return pl.pallas_call(
        stiffness_kernel,
        grid=(rves,),
        in_specs=[pl.BlockSpec(pieces.shape, lambda r: (0, 0, 0)), block, block],
        out_specs=block,
        out_shape=jax.ShapeDtypeStruct(slip_code.shape, jnp.float32),
    )(pieces, slip_code, grain_id)


def shift_cells(field, step):
    filler = jnp.zeros(field.shape[:-1] + (abs(step),), field.dtype)
    if step > 0:
        return jnp.concatenate([field[..., step:], filler], -1)
    return jnp.concatenate([filler, field[..., :step]], -1)


def local_dot(first, second):
    return jnp.sum(first * second, axis=(1, 2, 3))


def shards(macro_adjoint, slip_code, grain_id, grain_modulus, slip_softening, rve_spot):
    rve_count = slip_code.shape[0]
    cells = slip_code.shape[2]
    spot_count = macro_adjoint.shape[0] * lax.axis_size("hot")
    column = jnp.arange(cells) % RES
    upper_mask = (column != RES - 1).astype(jnp.float32)
    lower_mask = (column != 0).astype(jnp.float32)
    table = jnp.concatenate([grain_modulus[None, :], slip_softening.T], 0)

    def stiff_one(inputs):
        codes, grain_cells = inputs
        flat_codes = codes.reshape(-1)
        flat_grains = grain_cells.reshape(-1)
        onehot = (jnp.arange(GRAINS)[:, None] == flat_grains[None, :]).astype(jnp.float32)
        looked = jnp.dot(
            table, onehot, precision=lax.Precision.HIGHEST, preferred_element_type=jnp.float32
        )
        softening = jnp.zeros(flat_codes.shape, jnp.float32)
        for slip in range(SLIPS):
            active = (flat_codes // 2**slip % 2).astype(jnp.float32)
            softening = softening + active * looked[1 + slip]
        return (looked[0] / (1.0 + softening)).reshape(codes.shape)

    spot_onehot = (rve_spot[:, None] == jnp.arange(spot_count)[None, :]).astype(jnp.float32)
    parts, hot_me = axis_gather(macro_adjoint, "hot")
    if hot_me is None:
        all_strains = parts[0]
    else:
        local = macro_adjoint.shape[0]
        ordered = []
        for j in range(len(parts)):
            pick = [(hot_me ^ o) == j for o in range(len(parts))]
            block = parts[0]
            for o in range(1, len(parts)):
                block = jnp.where(pick[o], parts[o], block)
            ordered.append(block)
        all_strains = jnp.concatenate(ordered, 0)
    strains = jnp.dot(
        spot_onehot,
        all_strains,
        precision=lax.Precision.HIGHEST,
        preferred_element_type=jnp.float32,
    )
    stiff_slabs = stiffness(table, slip_code, grain_id)
    stiff = lax.all_to_all(stiff_slabs, "xc", 0, 1, tiled=True)
    mine = lax.axis_index("xc")
    strains = lax.dynamic_slice_in_dim(strains, mine, 1, 0)
    padded = padded_2(stiff, (("yb", 1),), 1)

    def squares(residual):
        return axis_sum(local_dot(residual, residual), "yb")

    near_xup = padded[:, 2:]
    near_xdn = padded[:, :-2]
    near_yup = shift_cells(stiff, RES)
    near_ydn = shift_cells(stiff, -RES)
    near_zup = shift_cells(stiff, 1) * upper_mask
    near_zdn = shift_cells(stiff, -1) * lower_mask
    face_xup = 0.5 * (stiff + near_xup)
    face_xdn = 0.5 * (stiff + near_xdn)
    face_yup = 0.5 * (stiff + near_yup)
    face_ydn = 0.5 * (stiff + near_ydn)
    face_zup = 0.5 * (stiff + near_zup)
    face_zdn = 0.5 * (stiff + near_zdn)
    diagonal_sum = (mass_term + face_xup + face_xdn + face_yup + face_ydn + face_zup + face_zdn)[
        :, None
    ]
    gradients = [
        0.5 * (near_xup - near_xdn),
        0.5 * (near_yup - near_ydn),
        0.5 * (near_zup - near_zdn),
    ]
    tensor = [
        [strains[:, 0], strains[:, 5], strains[:, 4]],
        [strains[:, 5], strains[:, 1], strains[:, 3]],
        [strains[:, 4], strains[:, 3], strains[:, 2]],
    ]
    source = jnp.stack(
        [
            gradients[0] * tensor[comp][0][:, None, None]
            + gradients[1] * tensor[comp][1][:, None, None]
            + gradients[2] * tensor[comp][2][:, None, None]
            for comp in range(3)
        ],
        1,
    )

    def expand(values):
        return values[:, None, None, None]

    def boundary_planes(value):
        size = lax.axis_size("yb")
        up = [(i, i + 1) for i in range(size - 1)]
        down = [(i + 1, i) for i in range(size - 1)]
        before = lax.ppermute(value[:, :, -1:], "yb", up)
        after = lax.ppermute(value[:, :, :1], "yb", down)
        return jnp.concatenate([before, after], 2)

    def operate(direction, edges):
        wide = jnp.concatenate([edges[:, :, :1], direction, edges[:, :, 1:]], 2)
        return (
            diagonal_sum * direction
            - face_xup[:, None] * wide[:, :, 2:]
            - face_xdn[:, None] * wide[:, :, :-2]
            - face_yup[:, None] * shift_cells(direction, RES)
            - face_ydn[:, None] * shift_cells(direction, -RES)
            - face_zup[:, None] * (shift_cells(direction, 1) * upper_mask)
            - face_zdn[:, None] * (shift_cells(direction, -1) * lower_mask)
        )

    def sum_and_planes(local, value):
        size = lax.axis_size("yb")
        if size != 4:
            return axis_sum(local, "yb"), boundary_planes(value)
        me = lax.axis_index("yb")
        even = me % 2 == 0
        count = local.shape[-1]
        first, final = value[0, :, 0, :], value[0, :, -1, :]
        row = jnp.pad(local, ((0, 0), (0, value.shape[-1] - count)))
        to_one = jnp.concatenate([jnp.where(even, final, first), row], 0)
        to_three = jnp.concatenate([jnp.where(even, first, final), row], 0)
        from_one = lax.ppermute(to_one, "yb", [(i, i ^ 1) for i in range(size)])
        from_three = lax.ppermute(to_three, "yb", [(i, i ^ 3) for i in range(size)])
        from_two = lax.ppermute(local, "yb", [(i, i ^ 2) for i in range(size)])
        total = (local + from_one[3:4, :count]) + (from_two + from_three[3:4, :count])
        before = jnp.where(me != 0, jnp.where(even, from_three[:3], from_one[:3]), 0.0)
        after = jnp.where(me != size - 1, jnp.where(even, from_one[:3], from_three[:3]), 0.0)
        return total, jnp.stack([before, after], 1)[None]

    answer = jnp.zeros_like(source)
    residual = source
    direction = source
    residual_edges = boundary_planes(source)
    direction_edges = residual_edges
    for step in range(ITERS):
        image = operate(direction, direction_edges)
        last = step + 1 == ITERS
        local = jnp.stack(
            [
                local_dot(direction, image),
                local_dot(residual, residual),
                local_dot(residual, image),
                local_dot(image, image),
            ],
            -1,
        )
        if last:
            sums = axis_sum(local, "yb")
        else:
            sums, image_edges = sum_and_planes(local, image)
        norm_now = sums[:, 1]
        alpha = norm_now / sums[:, 0]
        answer = answer + expand(alpha) * direction
        if last:
            break
        norm_next = norm_now - 2.0 * alpha * sums[:, 2] + alpha * alpha * sums[:, 3]
        beta = expand(norm_next / norm_now)
        residual = residual - expand(alpha) * image
        residual_edges = residual_edges - expand(alpha) * image_edges
        direction = residual + beta * direction
        direction_edges = residual_edges + beta * direction_edges
    volume = float(RES**3)
    stiff_part = jnp.sum(stiff, axis=(1, 2)) / volume
    moment = [
        [jnp.sum(answer[:, comp] * gradients[other], axis=(1, 2)) for other in range(3)]
        for comp in range(3)
    ]
    pairs = [(0, 0), (1, 1), (2, 2), (1, 2), (0, 2), (0, 1)]
    partial_here = jnp.stack(
        [
            stiff_part * strains[:, slot]
            - 0.5
            * (moment[pairs[slot][0]][pairs[slot][1]] + moment[pairs[slot][1]][pairs[slot][0]])
            / volume
            for slot in range(6)
        ],
        1,
    )
    per_spot = float(rve_count * lax.axis_size("hot") // spot_count)
    rve_one = axis_sum(partial_here, "yb")
    placed = (jnp.arange(rve_count)[:, None] == mine).astype(jnp.float32) * rve_one
    rve_totals = axis_sum(placed, "xc")
    spot_local = jnp.dot(
        spot_onehot.T,
        rve_totals,
        precision=lax.Precision.HIGHEST,
        preferred_element_type=jnp.float32,
    )
    owned = axis_reduce_scatter(spot_local, "hot")
    return (owned / per_spot, lax.all_to_all(answer, "xc", 2, 0, tiled=True))


def solution(mesh):
    hot, dom = mesh.shape["hot"], mesh.shape["dom"]
    rves_here = RVES // hot
    grouped = Mesh(mesh.devices.reshape(hot, dom // rves_here, rves_here), ("hot", "yb", "xc"))
    return jax.shard_map(
        shards,
        mesh=grouped,
        in_specs=(
            P("hot", None),
            P("hot", ("yb", "xc"), None),
            P("hot", ("yb", "xc"), None),
            P(),
            P(),
            P("hot"),
        ),
        out_specs=(P("hot", None), P("hot", None, ("yb", "xc"), None)),
        check_vma=False,
    )
```

```python
import jax
import jax.numpy as jnp
from jax import lax
from jax.experimental import pallas as pl
from jax.sharding import Mesh, PartitionSpec as P

RES = 64
SLIPS = 12
GRAINS = 64
ITERS = 8
RVES = 32


mass_term = 0.02


def padded_2(value, sides, width):
    for axis, dim in sides:
        devices, length = (lax.axis_size(axis), value.shape[dim])
        up = [(i, (i + 1) % devices) for i in range(devices - 1)]
        down = [(j, i) for i, j in up]
        last = lax.slice_in_dim(value, length - width, length, axis=dim)
        leading = lax.slice_in_dim(value, 0, width, axis=dim)
        before = lax.ppermute(last, axis, up)
        after = lax.ppermute(leading, axis, down)
        value = jnp.concatenate([before, value, after], axis=dim)
    return value


def xor_groups(size):
    bits = size.bit_length() - 1
    if size != 1 << bits:
        return None
    groups = [(0, 1)] if bits % 2 else []
    lo = bits % 2
    while lo < bits:
        groups.append((lo, 2))
        lo += 2
    return groups


def tree_sum(vals, nb):
    cur = dict(vals)
    for level in range(nb):
        cur = {o: v + cur[o | (1 << level)] for o, v in cur.items() if not o & (1 << level)}
    return cur[0]


def axis_sum(value, axis):
    size = lax.axis_size(axis)
    groups = xor_groups(size)
    if groups is None:
        return lax.psum(value, axis)
    for lo, nb in groups:
        vals = {0: value}
        for o in range(1, 1 << nb):
            mask = o << lo
            vals[o] = lax.ppermute(value, axis, [(i, i ^ mask) for i in range(size)])
        value = tree_sum(vals, nb)
    return value


def axis_gather(value, axis):
    size = lax.axis_size(axis)
    if xor_groups(size) is None:
        return [lax.all_gather(value, axis, axis=0, tiled=True)], None
    parts = [value] + [
        lax.ppermute(value, axis, [(i, i ^ o) for i in range(size)]) for o in range(1, size)
    ]
    return parts, lax.axis_index(axis)


def axis_reduce_scatter(value, axis):
    size = lax.axis_size(axis)
    if xor_groups(size) is None:
        return lax.psum_scatter(value, axis, scatter_dimension=0, tiled=True)
    me = lax.axis_index(axis)
    block = value.shape[0] // size
    nb = size.bit_length() - 1
    vals = {0: lax.dynamic_slice_in_dim(value, me * block, block, 0)}
    for o in range(1, size):
        wanted = lax.dynamic_slice_in_dim(value, (me ^ o) * block, block, 0)
        vals[o] = lax.ppermute(wanted, axis, [(i, i ^ o) for i in range(size)])
    return tree_sum(vals, nb)


CHUNK = 512


def stiffness_kernel(pieces_ref, codes_ref, grains_ref, out_ref):
    rows = pieces_ref.shape[1]

    def chunk(c, carry):
        at = pl.multiple_of(c * CHUNK, CHUNK)
        for plane in range(codes_ref.shape[1]):
            grains = grains_ref[0, plane : plane + 1, pl.ds(at, CHUNK)]
            codes = codes_ref[0, plane : plane + 1, pl.ds(at, CHUNK)]
            onehot = (lax.broadcasted_iota(jnp.int32, (GRAINS, CHUNK), 0) == grains).astype(jnp.bfloat16)
            looked = jnp.dot(pieces_ref[0], onehot, preferred_element_type=jnp.float32)
            looked = looked + jnp.dot(pieces_ref[1], onehot, preferred_element_type=jnp.float32)
            looked = looked + jnp.dot(pieces_ref[2], onehot, preferred_element_type=jnp.float32)
            softening = jnp.zeros((1, CHUNK), jnp.float32)
            for slip in range(SLIPS):
                active = ((codes >> slip) & 1).astype(jnp.float32)
                softening = softening + active * looked[1 + slip : 2 + slip, :]
            out_ref[0, plane : plane + 1, pl.ds(at, CHUNK)] = looked[0:1, :] / (1.0 + softening)
        return carry

    lax.fori_loop(0, codes_ref.shape[2] // CHUNK, chunk, 0)
    del rows


def stiffness(table, slip_code, grain_id):
    high = lax.reduce_precision(table, exponent_bits=8, mantissa_bits=7)
    rest = table - high
    middle = lax.reduce_precision(rest, exponent_bits=8, mantissa_bits=7)
    low = rest - middle
    pieces = jnp.stack([high, middle, low]).astype(jnp.bfloat16)
    pieces = jnp.pad(pieces, ((0, 0), (0, 16 - table.shape[0]), (0, 0)))
    rves, planes, cells = slip_code.shape
    block = pl.BlockSpec((1, planes, cells), lambda r: (r, 0, 0))
    return pl.pallas_call(
        stiffness_kernel,
        grid=(rves,),
        in_specs=[pl.BlockSpec(pieces.shape, lambda r: (0, 0, 0)), block, block],
        out_specs=block,
        out_shape=jax.ShapeDtypeStruct(slip_code.shape, jnp.float32),
    )(pieces, slip_code, grain_id)


def shift_cells(field, step):
    filler = jnp.zeros(field.shape[:-1] + (abs(step),), field.dtype)
    if step > 0:
        return jnp.concatenate([field[..., step:], filler], -1)
    return jnp.concatenate([filler, field[..., :step]], -1)


def local_dot(first, second):
    return jnp.sum(first * second, axis=(1, 2, 3))


def shards(macro_adjoint, slip_code, grain_id, grain_modulus, slip_softening, rve_spot):
    rve_count = slip_code.shape[0]
    cells = slip_code.shape[2]
    spot_count = macro_adjoint.shape[0] * lax.axis_size("hot")
    column = jnp.arange(cells) % RES
    upper_mask = (column != RES - 1).astype(jnp.float32)
    lower_mask = (column != 0).astype(jnp.float32)
    table = jnp.concatenate([grain_modulus[None, :], slip_softening.T], 0)

    def stiff_one(inputs):
        codes, grain_cells = inputs
        flat_codes = codes.reshape(-1)
        flat_grains = grain_cells.reshape(-1)
        onehot = (jnp.arange(GRAINS)[:, None] == flat_grains[None, :]).astype(jnp.float32)
        looked = jnp.dot(
            table, onehot, precision=lax.Precision.HIGHEST, preferred_element_type=jnp.float32
        )
        softening = jnp.zeros(flat_codes.shape, jnp.float32)
        for slip in range(SLIPS):
            active = (flat_codes // 2**slip % 2).astype(jnp.float32)
            softening = softening + active * looked[1 + slip]
        return (looked[0] / (1.0 + softening)).reshape(codes.shape)

    spot_onehot = (rve_spot[:, None] == jnp.arange(spot_count)[None, :]).astype(jnp.float32)
    parts, hot_me = axis_gather(macro_adjoint, "hot")
    if hot_me is None:
        all_strains = parts[0]
    else:
        local = macro_adjoint.shape[0]
        ordered = []
        for j in range(len(parts)):
            pick = [(hot_me ^ o) == j for o in range(len(parts))]
            block = parts[0]
            for o in range(1, len(parts)):
                block = jnp.where(pick[o], parts[o], block)
            ordered.append(block)
        all_strains = jnp.concatenate(ordered, 0)
    strains = jnp.dot(
        spot_onehot,
        all_strains,
        precision=lax.Precision.HIGHEST,
        preferred_element_type=jnp.float32,
    )
    stiff_slabs = stiffness(table, slip_code, grain_id)
    stiff = lax.all_to_all(stiff_slabs, "xc", 0, 1, tiled=True)
    mine = lax.axis_index("xc")
    strains = lax.dynamic_slice_in_dim(strains, mine, 1, 0)
    padded = padded_2(stiff, (("yb", 1),), 2)
    wide = padded[:, 1:-1]
    wide_xup, wide_xdn = padded[:, 2:], padded[:, :-2]
    wide_yup, wide_ydn = shift_cells(wide, RES), shift_cells(wide, -RES)
    wide_zup, wide_zdn = shift_cells(wide, 1) * upper_mask, shift_cells(wide, -1) * lower_mask

    def inner(planes):
        return planes[:, 1:-1]

    near_xup, near_xdn = inner(wide_xup), inner(wide_xdn)
    near_yup, near_ydn = inner(wide_yup), inner(wide_ydn)
    near_zup, near_zdn = inner(wide_zup), inner(wide_zdn)
    face_xup = 0.5 * (stiff + near_xup)
    face_xdn = 0.5 * (stiff + near_xdn)
    face_yup = 0.5 * (stiff + near_yup)
    face_ydn = 0.5 * (stiff + near_ydn)
    face_zup = 0.5 * (stiff + near_zup)
    face_zdn = 0.5 * (stiff + near_zdn)
    diagonal_sum = (mass_term + face_xup + face_xdn + face_yup + face_ydn + face_zup + face_zdn)[
        :, None
    ]
    wide_gradients = [
        0.5 * (wide_xup - wide_xdn),
        0.5 * (wide_yup - wide_ydn),
        0.5 * (wide_zup - wide_zdn),
    ]
    gradients = [inner(g) for g in wide_gradients]
    tensor = [
        [strains[:, 0], strains[:, 5], strains[:, 4]],
        [strains[:, 5], strains[:, 1], strains[:, 3]],
        [strains[:, 4], strains[:, 3], strains[:, 2]],
    ]
    wide_source = jnp.stack(
        [
            wide_gradients[0] * tensor[comp][0][:, None, None]
            + wide_gradients[1] * tensor[comp][1][:, None, None]
            + wide_gradients[2] * tensor[comp][2][:, None, None]
            for comp in range(3)
        ],
        1,
    )
    source = wide_source[:, :, 1:-1]
    plane_block = lax.axis_index("yb")
    source_edges = jnp.concatenate(
        [
            jnp.where(plane_block != 0, wide_source[:, :, :1], 0.0),
            jnp.where(plane_block != lax.axis_size("yb") - 1, wide_source[:, :, -1:], 0.0),
        ],
        2,
    )

    def expand(values):
        return values[:, None, None, None]

    def boundary_planes(value):
        size = lax.axis_size("yb")
        up = [(i, i + 1) for i in range(size - 1)]
        down = [(i + 1, i) for i in range(size - 1)]
        before = lax.ppermute(value[:, :, -1:], "yb", up)
        after = lax.ppermute(value[:, :, :1], "yb", down)
        return jnp.concatenate([before, after], 2)

    def operate(direction, edges):
        wide = jnp.concatenate([edges[:, :, :1], direction, edges[:, :, 1:]], 2)
        return (
            diagonal_sum * direction
            - face_xup[:, None] * wide[:, :, 2:]
            - face_xdn[:, None] * wide[:, :, :-2]
            - face_yup[:, None] * shift_cells(direction, RES)
            - face_ydn[:, None] * shift_cells(direction, -RES)
            - face_zup[:, None] * (shift_cells(direction, 1) * upper_mask)
            - face_zdn[:, None] * (shift_cells(direction, -1) * lower_mask)
        )

    answer = jnp.zeros_like(source)
    residual = source
    direction = source
    residual_edges = source_edges
    direction_edges = residual_edges
    for step in range(ITERS):
        image = operate(direction, direction_edges)
        last = step + 1 == ITERS
        if not last:
            image_edges = boundary_planes(image)
        terms = [
            local_dot(direction, image),
            local_dot(residual, residual),
            local_dot(residual, image),
            local_dot(image, image),
        ]
        if last:
            for held in (answer, direction):
                terms += [
                    jnp.sum(held[:, comp] * gradients[other], axis=(1, 2))
                    for comp in range(3)
                    for other in range(3)
                ]
            terms.append(jnp.sum(stiff, axis=(1, 2)))
        local = jnp.stack(terms, -1)
        sums = axis_sum(local, "yb")
        norm_now = sums[:, 1]
        alpha = norm_now / sums[:, 0]
        answer = answer + expand(alpha) * direction
        if last:
            break
        norm_next = norm_now - 2.0 * alpha * sums[:, 2] + alpha * alpha * sums[:, 3]
        beta = expand(norm_next / norm_now)
        residual = residual - expand(alpha) * image
        residual_edges = residual_edges - expand(alpha) * image_edges
        direction = residual + beta * direction
        direction_edges = residual_edges + beta * direction_edges
    volume = float(RES**3)
    stiff_part = sums[:, 22] / volume
    moment = [
        [sums[:, 4 + 3 * comp + other] + alpha * sums[:, 13 + 3 * comp + other] for other in range(3)]
        for comp in range(3)
    ]
    pairs = [(0, 0), (1, 1), (2, 2), (1, 2), (0, 2), (0, 1)]
    rve_one = jnp.stack(
        [
            stiff_part * strains[:, slot]
            - 0.5
            * (moment[pairs[slot][0]][pairs[slot][1]] + moment[pairs[slot][1]][pairs[slot][0]])
            / volume
            for slot in range(6)
        ],
        1,
    )
    per_spot = float(rve_count * lax.axis_size("hot") // spot_count)
    placed = (jnp.arange(rve_count)[:, None] == mine).astype(jnp.float32) * rve_one
    rve_totals = axis_sum(placed, "xc")
    spot_local = jnp.dot(
        spot_onehot.T,
        rve_totals,
        precision=lax.Precision.HIGHEST,
        preferred_element_type=jnp.float32,
    )
    owned = axis_reduce_scatter(spot_local, "hot")
    return (owned / per_spot, lax.all_to_all(answer, "xc", 2, 0, tiled=True))


def solution(mesh):
    hot, dom = mesh.shape["hot"], mesh.shape["dom"]
    rves_here = RVES // hot
    grouped = Mesh(mesh.devices.reshape(hot, dom // rves_here, rves_here), ("hot", "yb", "xc"))
    return jax.shard_map(
        shards,
        mesh=grouped,
        in_specs=(
            P("hot", None),
            P("hot", ("yb", "xc"), None),
            P("hot", ("yb", "xc"), None),
            P(),
            P(),
            P("hot"),
        ),
        out_specs=(P("hot", None), P("hot", None, ("yb", "xc"), None)),
        check_vma=False,
    )
```

```python
import jax
import jax.numpy as jnp
from jax import lax
from jax.experimental import pallas as pl
from jax.sharding import Mesh, PartitionSpec as P

RES = 64
SLIPS = 12
GRAINS = 64
ITERS = 8
RVES = 32


mass_term = 0.02


def padded_2(value, sides, width):
    for axis, dim in sides:
        devices, length = (lax.axis_size(axis), value.shape[dim])
        up = [(i, (i + 1) % devices) for i in range(devices - 1)]
        down = [(j, i) for i, j in up]
        last = lax.slice_in_dim(value, length - width, length, axis=dim)
        leading = lax.slice_in_dim(value, 0, width, axis=dim)
        before = lax.ppermute(last, axis, up)
        after = lax.ppermute(leading, axis, down)
        value = jnp.concatenate([before, value, after], axis=dim)
    return value


def xor_groups(size):
    bits = size.bit_length() - 1
    if size != 1 << bits:
        return None
    groups = [(0, 1)] if bits % 2 else []
    lo = bits % 2
    while lo < bits:
        groups.append((lo, 2))
        lo += 2
    return groups


def tree_sum(vals, nb):
    cur = dict(vals)
    for level in range(nb):
        cur = {o: v + cur[o | (1 << level)] for o, v in cur.items() if not o & (1 << level)}
    return cur[0]


def axis_sum(value, axis):
    size = lax.axis_size(axis)
    groups = xor_groups(size)
    if groups is None:
        return lax.psum(value, axis)
    for lo, nb in groups:
        vals = {0: value}
        for o in range(1, 1 << nb):
            mask = o << lo
            vals[o] = lax.ppermute(value, axis, [(i, i ^ mask) for i in range(size)])
        value = tree_sum(vals, nb)
    return value


def axis_gather(value, axis):
    size = lax.axis_size(axis)
    if xor_groups(size) is None:
        return [lax.all_gather(value, axis, axis=0, tiled=True)], None
    parts = [value] + [
        lax.ppermute(value, axis, [(i, i ^ o) for i in range(size)]) for o in range(1, size)
    ]
    return parts, lax.axis_index(axis)


def axis_reduce_scatter(value, axis):
    size = lax.axis_size(axis)
    if xor_groups(size) is None:
        return lax.psum_scatter(value, axis, scatter_dimension=0, tiled=True)
    me = lax.axis_index(axis)
    block = value.shape[0] // size
    nb = size.bit_length() - 1
    vals = {0: lax.dynamic_slice_in_dim(value, me * block, block, 0)}
    for o in range(1, size):
        wanted = lax.dynamic_slice_in_dim(value, (me ^ o) * block, block, 0)
        vals[o] = lax.ppermute(wanted, axis, [(i, i ^ o) for i in range(size)])
    return tree_sum(vals, nb)


CHUNK = 512


def stiffness_kernel(pieces_ref, codes_ref, grains_ref, out_ref):
    rows = pieces_ref.shape[1]

    def chunk(c, carry):
        at = pl.multiple_of(c * CHUNK, CHUNK)
        for plane in range(codes_ref.shape[1]):
            grains = grains_ref[0, plane : plane + 1, pl.ds(at, CHUNK)]
            codes = codes_ref[0, plane : plane + 1, pl.ds(at, CHUNK)]
            onehot = (lax.broadcasted_iota(jnp.int32, (GRAINS, CHUNK), 0) == grains).astype(jnp.bfloat16)
            looked = jnp.dot(pieces_ref[0], onehot, preferred_element_type=jnp.float32)
            looked = looked + jnp.dot(pieces_ref[1], onehot, preferred_element_type=jnp.float32)
            looked = looked + jnp.dot(pieces_ref[2], onehot, preferred_element_type=jnp.float32)
            softening = jnp.zeros((1, CHUNK), jnp.float32)
            for slip in range(SLIPS):
                active = ((codes >> slip) & 1).astype(jnp.float32)
                softening = softening + active * looked[1 + slip : 2 + slip, :]
            out_ref[0, plane : plane + 1, pl.ds(at, CHUNK)] = looked[0:1, :] / (1.0 + softening)
        return carry

    lax.fori_loop(0, codes_ref.shape[2] // CHUNK, chunk, 0)
    del rows


def stiffness(table, slip_code, grain_id):
    high = lax.reduce_precision(table, exponent_bits=8, mantissa_bits=7)
    rest = table - high
    middle = lax.reduce_precision(rest, exponent_bits=8, mantissa_bits=7)
    low = rest - middle
    pieces = jnp.stack([high, middle, low]).astype(jnp.bfloat16)
    pieces = jnp.pad(pieces, ((0, 0), (0, 16 - table.shape[0]), (0, 0)))
    rves, planes, cells = slip_code.shape
    block = pl.BlockSpec((1, planes, cells), lambda r: (r, 0, 0))
    return pl.pallas_call(
        stiffness_kernel,
        grid=(rves,),
        in_specs=[pl.BlockSpec(pieces.shape, lambda r: (0, 0, 0)), block, block],
        out_specs=block,
        out_shape=jax.ShapeDtypeStruct(slip_code.shape, jnp.float32),
    )(pieces, slip_code, grain_id)


def shift_cells(field, step):
    filler = jnp.zeros(field.shape[:-1] + (abs(step),), field.dtype)
    if step > 0:
        return jnp.concatenate([field[..., step:], filler], -1)
    return jnp.concatenate([filler, field[..., :step]], -1)


def local_dot(first, second):
    return jnp.sum(first * second, axis=(1, 2, 3))


def shards(macro_adjoint, slip_code, grain_id, grain_modulus, slip_softening, rve_spot):
    rve_count = slip_code.shape[0]
    cells = slip_code.shape[2]
    spot_count = macro_adjoint.shape[0] * lax.axis_size("hot")
    column = jnp.arange(cells) % RES
    upper_mask = (column != RES - 1).astype(jnp.float32)
    lower_mask = (column != 0).astype(jnp.float32)
    table = jnp.concatenate([grain_modulus[None, :], slip_softening.T], 0)

    def stiff_one(inputs):
        codes, grain_cells = inputs
        flat_codes = codes.reshape(-1)
        flat_grains = grain_cells.reshape(-1)
        onehot = (jnp.arange(GRAINS)[:, None] == flat_grains[None, :]).astype(jnp.float32)
        looked = jnp.dot(
            table, onehot, precision=lax.Precision.HIGHEST, preferred_element_type=jnp.float32
        )
        softening = jnp.zeros(flat_codes.shape, jnp.float32)
        for slip in range(SLIPS):
            active = (flat_codes // 2**slip % 2).astype(jnp.float32)
            softening = softening + active * looked[1 + slip]
        return (looked[0] / (1.0 + softening)).reshape(codes.shape)

    spot_onehot = (rve_spot[:, None] == jnp.arange(spot_count)[None, :]).astype(jnp.float32)
    parts, hot_me = axis_gather(macro_adjoint, "hot")
    if hot_me is None:
        all_strains = parts[0]
    else:
        local = macro_adjoint.shape[0]
        ordered = []
        for j in range(len(parts)):
            pick = [(hot_me ^ o) == j for o in range(len(parts))]
            block = parts[0]
            for o in range(1, len(parts)):
                block = jnp.where(pick[o], parts[o], block)
            ordered.append(block)
        all_strains = jnp.concatenate(ordered, 0)
    strains = jnp.dot(
        spot_onehot,
        all_strains,
        precision=lax.Precision.HIGHEST,
        preferred_element_type=jnp.float32,
    )
    stiff_slabs = stiffness(table, slip_code, grain_id)
    stiff = lax.all_to_all(stiff_slabs, "xc", 0, 1, tiled=True)
    mine = lax.axis_index("xc")
    strains = lax.dynamic_slice_in_dim(strains, mine, 1, 0)
    padded = padded_2(stiff, (("yb", 1),), 2)
    wide = padded[:, 1:-1]
    wide_xup, wide_xdn = padded[:, 2:], padded[:, :-2]
    wide_yup, wide_ydn = shift_cells(wide, RES), shift_cells(wide, -RES)
    wide_zup, wide_zdn = shift_cells(wide, 1) * upper_mask, shift_cells(wide, -1) * lower_mask

    def inner(planes):
        return planes[:, 1:-1]

    near_xup, near_xdn = inner(wide_xup), inner(wide_xdn)
    near_yup, near_ydn = inner(wide_yup), inner(wide_ydn)
    near_zup, near_zdn = inner(wide_zup), inner(wide_zdn)
    face_xup = 0.5 * (stiff + near_xup)
    face_xdn = 0.5 * (stiff + near_xdn)
    face_yup = 0.5 * (stiff + near_yup)
    face_ydn = 0.5 * (stiff + near_ydn)
    face_zup = 0.5 * (stiff + near_zup)
    face_zdn = 0.5 * (stiff + near_zdn)
    diagonal_sum = (mass_term + face_xup + face_xdn + face_yup + face_ydn + face_zup + face_zdn)[
        :, None
    ]
    wide_gradients = [
        0.5 * (wide_xup - wide_xdn),
        0.5 * (wide_yup - wide_ydn),
        0.5 * (wide_zup - wide_zdn),
    ]
    gradients = [inner(g) for g in wide_gradients]
    tensor = [
        [strains[:, 0], strains[:, 5], strains[:, 4]],
        [strains[:, 5], strains[:, 1], strains[:, 3]],
        [strains[:, 4], strains[:, 3], strains[:, 2]],
    ]
    wide_source = jnp.stack(
        [
            wide_gradients[0] * tensor[comp][0][:, None, None]
            + wide_gradients[1] * tensor[comp][1][:, None, None]
            + wide_gradients[2] * tensor[comp][2][:, None, None]
            for comp in range(3)
        ],
        1,
    )
    source = wide_source[:, :, 1:-1]
    plane_block = lax.axis_index("yb")
    source_edges = jnp.concatenate(
        [
            jnp.where(plane_block != 0, wide_source[:, :, :1], 0.0),
            jnp.where(plane_block != lax.axis_size("yb") - 1, wide_source[:, :, -1:], 0.0),
        ],
        2,
    )

    def expand(values):
        return values[:, None, None, None]

    def boundary_planes(value):
        size = lax.axis_size("yb")
        up = [(i, i + 1) for i in range(size - 1)]
        down = [(i + 1, i) for i in range(size - 1)]
        before = lax.ppermute(value[:, :, -1:], "yb", up)
        after = lax.ppermute(value[:, :, :1], "yb", down)
        return jnp.concatenate([before, after], 2)

    def operate(direction, edges):
        wide = jnp.concatenate([edges[:, :, :1], direction, edges[:, :, 1:]], 2)
        return (
            diagonal_sum * direction
            - face_xup[:, None] * wide[:, :, 2:]
            - face_xdn[:, None] * wide[:, :, :-2]
            - face_yup[:, None] * shift_cells(direction, RES)
            - face_ydn[:, None] * shift_cells(direction, -RES)
            - face_zup[:, None] * (shift_cells(direction, 1) * upper_mask)
            - face_zdn[:, None] * (shift_cells(direction, -1) * lower_mask)
        )

    answer = jnp.zeros_like(source)
    residual = source
    direction = source
    residual_edges = source_edges
    direction_edges = residual_edges
    for step in range(ITERS):
        image = operate(direction, direction_edges)
        last = step + 1 == ITERS
        if not last:
            image_edges = boundary_planes(image)
        terms = [
            local_dot(direction, image),
            local_dot(residual, residual),
            local_dot(residual, image),
            local_dot(image, image),
        ]
        if last:
            for held in (answer, direction):
                terms += [
                    jnp.sum(held[:, comp] * gradients[other], axis=(1, 2))
                    for comp in range(3)
                    for other in range(3)
                ]
            terms.append(jnp.sum(stiff, axis=(1, 2)))
        local = jnp.stack(terms, -1)
        sums = axis_sum(local, "yb")
        norm_now = sums[:, 1]
        alpha = norm_now / sums[:, 0]
        answer = answer + expand(alpha) * direction
        if last:
            break
        norm_next = norm_now - 2.0 * alpha * sums[:, 2] + alpha * alpha * sums[:, 3]
        beta = expand(norm_next / norm_now)
        residual = residual - expand(alpha) * image
        residual_edges = residual_edges - expand(alpha) * image_edges
        direction = residual + beta * direction
        direction_edges = residual_edges + beta * direction_edges
    volume = float(RES**3)
    moments = sums[:, 4:13] + alpha[:, None] * sums[:, 13:22]
    pair_sum = jnp.take(moments, jnp.array([0, 4, 8, 5, 2, 1]), axis=1) + jnp.take(
        moments, jnp.array([0, 4, 8, 7, 6, 3]), axis=1
    )
    rve_one = sums[:, 22:23] / volume * strains - 0.5 * pair_sum / volume
    per_spot = float(rve_count * lax.axis_size("hot") // spot_count)
    placed = (jnp.arange(rve_count)[:, None] == mine).astype(jnp.float32) * rve_one
    rve_totals = axis_sum(placed, "xc")
    spot_local = jnp.dot(
        spot_onehot.T,
        rve_totals,
        precision=lax.Precision.HIGHEST,
        preferred_element_type=jnp.float32,
    )
    owned = axis_reduce_scatter(spot_local, "hot")
    return (owned / per_spot, lax.all_to_all(answer, "xc", 2, 0, tiled=True))


def solution(mesh):
    hot, dom = mesh.shape["hot"], mesh.shape["dom"]
    rves_here = RVES // hot
    grouped = Mesh(mesh.devices.reshape(hot, dom // rves_here, rves_here), ("hot", "yb", "xc"))
    return jax.shard_map(
        shards,
        mesh=grouped,
        in_specs=(
            P("hot", None),
            P("hot", ("yb", "xc"), None),
            P("hot", ("yb", "xc"), None),
            P(),
            P(),
            P("hot"),
        ),
        out_specs=(P("hot", None), P("hot", None, ("yb", "xc"), None)),
        check_vma=False,
    )
```

```python
import jax
import jax.numpy as jnp
from jax import lax
from jax.experimental import pallas as pl
from jax.sharding import Mesh, PartitionSpec as P

RES = 64
SLIPS = 12
GRAINS = 64
ITERS = 8
RVES = 32


mass_term = 0.02


def padded_2(value, sides, width):
    for axis, dim in sides:
        devices, length = (lax.axis_size(axis), value.shape[dim])
        up = [(i, (i + 1) % devices) for i in range(devices - 1)]
        down = [(j, i) for i, j in up]
        last = lax.slice_in_dim(value, length - width, length, axis=dim)
        leading = lax.slice_in_dim(value, 0, width, axis=dim)
        before = lax.ppermute(last, axis, up)
        after = lax.ppermute(leading, axis, down)
        value = jnp.concatenate([before, value, after], axis=dim)
    return value


def xor_groups(size):
    bits = size.bit_length() - 1
    if size != 1 << bits:
        return None
    groups = [(0, 1)] if bits % 2 else []
    lo = bits % 2
    while lo < bits:
        groups.append((lo, 2))
        lo += 2
    return groups


def tree_sum(vals, nb):
    cur = dict(vals)
    for level in range(nb):
        cur = {o: v + cur[o | (1 << level)] for o, v in cur.items() if not o & (1 << level)}
    return cur[0]


def axis_sum(value, axis):
    size = lax.axis_size(axis)
    groups = xor_groups(size)
    if groups is None:
        return lax.psum(value, axis)
    for lo, nb in groups:
        vals = {0: value}
        for o in range(1, 1 << nb):
            mask = o << lo
            vals[o] = lax.ppermute(value, axis, [(i, i ^ mask) for i in range(size)])
        value = tree_sum(vals, nb)
    return value


def axis_gather(value, axis):
    size = lax.axis_size(axis)
    if xor_groups(size) is None:
        return [lax.all_gather(value, axis, axis=0, tiled=True)], None
    parts = [value] + [
        lax.ppermute(value, axis, [(i, i ^ o) for i in range(size)]) for o in range(1, size)
    ]
    return parts, lax.axis_index(axis)


def axis_reduce_scatter(value, axis):
    size = lax.axis_size(axis)
    if xor_groups(size) is None:
        return lax.psum_scatter(value, axis, scatter_dimension=0, tiled=True)
    me = lax.axis_index(axis)
    block = value.shape[0] // size
    nb = size.bit_length() - 1
    vals = {0: lax.dynamic_slice_in_dim(value, me * block, block, 0)}
    for o in range(1, size):
        wanted = lax.dynamic_slice_in_dim(value, (me ^ o) * block, block, 0)
        vals[o] = lax.ppermute(wanted, axis, [(i, i ^ o) for i in range(size)])
    return tree_sum(vals, nb)


CHUNK = 512


def stiffness_kernel(pieces_ref, codes_ref, grains_ref, out_ref):
    rows = pieces_ref.shape[1]

    def chunk(c, carry):
        at = pl.multiple_of(c * CHUNK, CHUNK)
        for plane in range(codes_ref.shape[1]):
            grains = grains_ref[0, plane : plane + 1, pl.ds(at, CHUNK)]
            codes = codes_ref[0, plane : plane + 1, pl.ds(at, CHUNK)]
            onehot = (lax.broadcasted_iota(jnp.int32, (GRAINS, CHUNK), 0) == grains).astype(jnp.bfloat16)
            looked = jnp.dot(pieces_ref[0], onehot, preferred_element_type=jnp.float32)
            looked = looked + jnp.dot(pieces_ref[1], onehot, preferred_element_type=jnp.float32)
            looked = looked + jnp.dot(pieces_ref[2], onehot, preferred_element_type=jnp.float32)
            softening = jnp.zeros((1, CHUNK), jnp.float32)
            for slip in range(SLIPS):
                active = ((codes >> slip) & 1).astype(jnp.float32)
                softening = softening + active * looked[1 + slip : 2 + slip, :]
            out_ref[0, plane : plane + 1, pl.ds(at, CHUNK)] = looked[0:1, :] / (1.0 + softening)
        return carry

    lax.fori_loop(0, codes_ref.shape[2] // CHUNK, chunk, 0)
    del rows


def stiffness(table, slip_code, grain_id):
    high = lax.reduce_precision(table, exponent_bits=8, mantissa_bits=7)
    rest = table - high
    middle = lax.reduce_precision(rest, exponent_bits=8, mantissa_bits=7)
    low = rest - middle
    pieces = jnp.stack([high, middle, low]).astype(jnp.bfloat16)
    pieces = jnp.pad(pieces, ((0, 0), (0, 16 - table.shape[0]), (0, 0)))
    rves, planes, cells = slip_code.shape
    block = pl.BlockSpec((1, planes, cells), lambda r: (r, 0, 0))
    return pl.pallas_call(
        stiffness_kernel,
        grid=(rves,),
        in_specs=[pl.BlockSpec(pieces.shape, lambda r: (0, 0, 0)), block, block],
        out_specs=block,
        out_shape=jax.ShapeDtypeStruct(slip_code.shape, jnp.float32),
    )(pieces, slip_code, grain_id)


def shift_cells(field, step):
    filler = jnp.zeros(field.shape[:-1] + (abs(step),), field.dtype)
    if step > 0:
        return jnp.concatenate([field[..., step:], filler], -1)
    return jnp.concatenate([filler, field[..., :step]], -1)


def local_dot(first, second):
    return jnp.sum(first * second, axis=(1, 2, 3))


def shards(macro_adjoint, slip_code, grain_id, grain_modulus, slip_softening, rve_spot):
    rve_count = slip_code.shape[0]
    cells = slip_code.shape[2]
    spot_count = macro_adjoint.shape[0] * lax.axis_size("hot")
    column = jnp.arange(cells) % RES
    upper_mask = (column != RES - 1).astype(jnp.float32)
    lower_mask = (column != 0).astype(jnp.float32)
    table = jnp.concatenate([grain_modulus[None, :], slip_softening.T], 0)

    def stiff_one(inputs):
        codes, grain_cells = inputs
        flat_codes = codes.reshape(-1)
        flat_grains = grain_cells.reshape(-1)
        onehot = (jnp.arange(GRAINS)[:, None] == flat_grains[None, :]).astype(jnp.float32)
        looked = jnp.dot(
            table, onehot, precision=lax.Precision.HIGHEST, preferred_element_type=jnp.float32
        )
        softening = jnp.zeros(flat_codes.shape, jnp.float32)
        for slip in range(SLIPS):
            active = (flat_codes // 2**slip % 2).astype(jnp.float32)
            softening = softening + active * looked[1 + slip]
        return (looked[0] / (1.0 + softening)).reshape(codes.shape)

    spot_onehot = (rve_spot[:, None] == jnp.arange(spot_count)[None, :]).astype(jnp.float32)
    parts, hot_me = axis_gather(macro_adjoint, "hot")
    if hot_me is None:
        all_strains = parts[0]
    else:
        local = macro_adjoint.shape[0]
        ordered = []
        for j in range(len(parts)):
            pick = [(hot_me ^ o) == j for o in range(len(parts))]
            block = parts[0]
            for o in range(1, len(parts)):
                block = jnp.where(pick[o], parts[o], block)
            ordered.append(block)
        all_strains = jnp.concatenate(ordered, 0)
    strains = jnp.dot(
        spot_onehot,
        all_strains,
        precision=lax.Precision.HIGHEST,
        preferred_element_type=jnp.float32,
    )
    stiff_slabs = stiffness(table, slip_code, grain_id)
    stiff = lax.all_to_all(stiff_slabs, "xc", 0, 1, tiled=True)
    mine = lax.axis_index("xc")
    strains = lax.dynamic_slice_in_dim(strains, mine, 1, 0)
    padded = padded_2(stiff, (("yb", 1),), 2)
    wide = padded[:, 1:-1]
    wide_xup, wide_xdn = padded[:, 2:], padded[:, :-2]
    wide_yup, wide_ydn = shift_cells(wide, RES), shift_cells(wide, -RES)
    wide_zup, wide_zdn = shift_cells(wide, 1) * upper_mask, shift_cells(wide, -1) * lower_mask

    def inner(planes):
        return planes[:, 1:-1]

    near_xup, near_xdn = inner(wide_xup), inner(wide_xdn)
    near_yup, near_ydn = inner(wide_yup), inner(wide_ydn)
    near_zup, near_zdn = inner(wide_zup), inner(wide_zdn)
    face_xup = 0.5 * (stiff + near_xup)
    face_xdn = 0.5 * (stiff + near_xdn)
    face_yup = 0.5 * (stiff + near_yup)
    face_ydn = 0.5 * (stiff + near_ydn)
    face_zup = 0.5 * (stiff + near_zup)
    face_zdn = 0.5 * (stiff + near_zdn)
    diagonal_sum = (mass_term + face_xup + face_xdn + face_yup + face_ydn + face_zup + face_zdn)[
        :, None
    ]
    wide_gradients = [
        0.5 * (wide_xup - wide_xdn),
        0.5 * (wide_yup - wide_ydn),
        0.5 * (wide_zup - wide_zdn),
    ]
    gradients = [inner(g) for g in wide_gradients]
    tensor = [
        [strains[:, 0], strains[:, 5], strains[:, 4]],
        [strains[:, 5], strains[:, 1], strains[:, 3]],
        [strains[:, 4], strains[:, 3], strains[:, 2]],
    ]
    wide_source = jnp.stack(
        [
            wide_gradients[0] * tensor[comp][0][:, None, None]
            + wide_gradients[1] * tensor[comp][1][:, None, None]
            + wide_gradients[2] * tensor[comp][2][:, None, None]
            for comp in range(3)
        ],
        1,
    )
    source = wide_source[:, :, 1:-1]
    plane_block = lax.axis_index("yb")
    source_edges = jnp.concatenate(
        [
            jnp.where(plane_block != 0, wide_source[:, :, :1], 0.0),
            jnp.where(plane_block != lax.axis_size("yb") - 1, wide_source[:, :, -1:], 0.0),
        ],
        2,
    )

    def expand(values):
        return values[:, None, None, None]

    def boundary_planes(value):
        size = lax.axis_size("yb")
        up = [(i, i + 1) for i in range(size - 1)]
        down = [(i + 1, i) for i in range(size - 1)]
        before = lax.ppermute(value[:, :, -1:], "yb", up)
        after = lax.ppermute(value[:, :, :1], "yb", down)
        return jnp.concatenate([before, after], 2)

    def operate(direction, edges):
        wide = jnp.concatenate([edges[:, :, :1], direction, edges[:, :, 1:]], 2)
        return (
            diagonal_sum * direction
            - face_xup[:, None] * wide[:, :, 2:]
            - face_xdn[:, None] * wide[:, :, :-2]
            - face_yup[:, None] * shift_cells(direction, RES)
            - face_ydn[:, None] * shift_cells(direction, -RES)
            - face_zup[:, None] * (shift_cells(direction, 1) * upper_mask)
            - face_zdn[:, None] * (shift_cells(direction, -1) * lower_mask)
        )

    answer = jnp.zeros_like(source)
    residual = source
    direction = source
    residual_edges = source_edges
    direction_edges = residual_edges
    for step in range(ITERS):
        image = operate(direction, direction_edges)
        last = step + 1 == ITERS
        if not last:
            image_edges = boundary_planes(image)
        terms = [
            local_dot(direction, image),
            local_dot(residual, residual),
            local_dot(residual, image),
            local_dot(image, image),
        ]
        if last:
            for held in (answer, direction):
                terms += [
                    jnp.sum(held[:, comp] * gradients[other], axis=(1, 2))
                    for comp in range(3)
                    for other in range(3)
                ]
            terms.append(jnp.sum(stiff, axis=(1, 2)))
        local = jnp.stack(terms, -1)
        sums = axis_sum(local, "yb")
        norm_now = sums[:, 1]
        alpha = norm_now / sums[:, 0]
        if last:
            slab_answer = lax.all_to_all(answer, "xc", 2, 0, tiled=True)
            slab_direction = lax.all_to_all(direction, "xc", 2, 0, tiled=True)
            break
        answer = answer + expand(alpha) * direction
        norm_next = norm_now - 2.0 * alpha * sums[:, 2] + alpha * alpha * sums[:, 3]
        beta = expand(norm_next / norm_now)
        residual = residual - expand(alpha) * image
        residual_edges = residual_edges - expand(alpha) * image_edges
        direction = residual + beta * direction
        direction_edges = residual_edges + beta * direction_edges
    volume = float(RES**3)
    moments = sums[:, 4:13] + alpha[:, None] * sums[:, 13:22]
    pair_sum = jnp.take(moments, jnp.array([0, 4, 8, 5, 2, 1]), axis=1) + jnp.take(
        moments, jnp.array([0, 4, 8, 7, 6, 3]), axis=1
    )
    rve_one = sums[:, 22:23] / volume * strains - 0.5 * pair_sum / volume
    per_spot = float(rve_count * lax.axis_size("hot") // spot_count)
    placed = (jnp.arange(rve_count)[:, None] == mine).astype(jnp.float32) * jnp.concatenate(
        [rve_one, alpha[:, None]], 1
    )
    placed = axis_sum(placed, "xc")
    rve_totals, slab_alpha = placed[:, :6], placed[:, 6]
    spot_local = jnp.dot(
        spot_onehot.T,
        rve_totals,
        precision=lax.Precision.HIGHEST,
        preferred_element_type=jnp.float32,
    )
    owned = axis_reduce_scatter(spot_local, "hot")
    return (owned / per_spot, slab_answer + expand(slab_alpha) * slab_direction)


def solution(mesh):
    hot, dom = mesh.shape["hot"], mesh.shape["dom"]
    rves_here = RVES // hot
    grouped = Mesh(mesh.devices.reshape(hot, dom // rves_here, rves_here), ("hot", "yb", "xc"))
    return jax.shard_map(
        shards,
        mesh=grouped,
        in_specs=(
            P("hot", None),
            P("hot", ("yb", "xc"), None),
            P("hot", ("yb", "xc"), None),
            P(),
            P(),
            P("hot"),
        ),
        out_specs=(P("hot", None), P("hot", None, ("yb", "xc"), None)),
        check_vma=False,
    )
```

```python
import jax
import jax.numpy as jnp
from jax import lax
from jax.experimental import pallas as pl
from jax.sharding import Mesh, PartitionSpec as P

RES = 64
SLIPS = 12
GRAINS = 64
ITERS = 8
RVES = 32


mass_term = 0.02


def padded_2(value, sides, width):
    for axis, dim in sides:
        devices, length = (lax.axis_size(axis), value.shape[dim])
        up = [(i, (i + 1) % devices) for i in range(devices - 1)]
        down = [(j, i) for i, j in up]
        last = lax.slice_in_dim(value, length - width, length, axis=dim)
        leading = lax.slice_in_dim(value, 0, width, axis=dim)
        before = lax.ppermute(last, axis, up)
        after = lax.ppermute(leading, axis, down)
        value = jnp.concatenate([before, value, after], axis=dim)
    return value


def xor_groups(size):
    bits = size.bit_length() - 1
    if size != 1 << bits:
        return None
    groups = [(0, 1)] if bits % 2 else []
    lo = bits % 2
    while lo < bits:
        groups.append((lo, 2))
        lo += 2
    return groups


def tree_sum(vals, nb):
    cur = dict(vals)
    for level in range(nb):
        cur = {o: v + cur[o | (1 << level)] for o, v in cur.items() if not o & (1 << level)}
    return cur[0]


def axis_sum(value, axis):
    size = lax.axis_size(axis)
    groups = xor_groups(size)
    if groups is None:
        return lax.psum(value, axis)
    for lo, nb in groups:
        vals = {0: value}
        for o in range(1, 1 << nb):
            mask = o << lo
            vals[o] = lax.ppermute(value, axis, [(i, i ^ mask) for i in range(size)])
        value = tree_sum(vals, nb)
    return value


def axis_gather(value, axis):
    size = lax.axis_size(axis)
    if xor_groups(size) is None:
        return [lax.all_gather(value, axis, axis=0, tiled=True)], None
    parts = [value] + [
        lax.ppermute(value, axis, [(i, i ^ o) for i in range(size)]) for o in range(1, size)
    ]
    return parts, lax.axis_index(axis)


def axis_reduce_scatter(value, axis):
    size = lax.axis_size(axis)
    if xor_groups(size) is None:
        return lax.psum_scatter(value, axis, scatter_dimension=0, tiled=True)
    me = lax.axis_index(axis)
    block = value.shape[0] // size
    nb = size.bit_length() - 1
    vals = {0: lax.dynamic_slice_in_dim(value, me * block, block, 0)}
    for o in range(1, size):
        wanted = lax.dynamic_slice_in_dim(value, (me ^ o) * block, block, 0)
        vals[o] = lax.ppermute(wanted, axis, [(i, i ^ o) for i in range(size)])
    return tree_sum(vals, nb)


CHUNK = 512


def stiffness_kernel(pieces_ref, codes_ref, grains_ref, out_ref):
    rows = pieces_ref.shape[1]

    def chunk(c, carry):
        at = pl.multiple_of(c * CHUNK, CHUNK)
        for plane in range(codes_ref.shape[1]):
            grains = grains_ref[0, plane : plane + 1, pl.ds(at, CHUNK)]
            codes = codes_ref[0, plane : plane + 1, pl.ds(at, CHUNK)]
            onehot = (lax.broadcasted_iota(jnp.int32, (GRAINS, CHUNK), 0) == grains).astype(jnp.bfloat16)
            looked = jnp.dot(pieces_ref[0], onehot, preferred_element_type=jnp.float32)
            looked = looked + jnp.dot(pieces_ref[1], onehot, preferred_element_type=jnp.float32)
            looked = looked + jnp.dot(pieces_ref[2], onehot, preferred_element_type=jnp.float32)
            softening = jnp.zeros((1, CHUNK), jnp.float32)
            for slip in range(SLIPS):
                active = ((codes >> slip) & 1).astype(jnp.float32)
                softening = softening + active * looked[1 + slip : 2 + slip, :]
            out_ref[0, plane : plane + 1, pl.ds(at, CHUNK)] = looked[0:1, :] / (1.0 + softening)
        return carry

    lax.fori_loop(0, codes_ref.shape[2] // CHUNK, chunk, 0)
    del rows


def stiffness(table, slip_code, grain_id):
    high = lax.reduce_precision(table, exponent_bits=8, mantissa_bits=7)
    rest = table - high
    middle = lax.reduce_precision(rest, exponent_bits=8, mantissa_bits=7)
    low = rest - middle
    pieces = jnp.stack([high, middle, low]).astype(jnp.bfloat16)
    pieces = jnp.pad(pieces, ((0, 0), (0, 16 - table.shape[0]), (0, 0)))
    rves, planes, cells = slip_code.shape
    block = pl.BlockSpec((1, planes, cells), lambda r: (r, 0, 0))
    return pl.pallas_call(
        stiffness_kernel,
        grid=(rves,),
        in_specs=[pl.BlockSpec(pieces.shape, lambda r: (0, 0, 0)), block, block],
        out_specs=block,
        out_shape=jax.ShapeDtypeStruct(slip_code.shape, jnp.float32),
    )(pieces, slip_code, grain_id)


def shift_cells(field, step):
    filler = jnp.zeros(field.shape[:-1] + (abs(step),), field.dtype)
    if step > 0:
        return jnp.concatenate([field[..., step:], filler], -1)
    return jnp.concatenate([filler, field[..., :step]], -1)


def local_dot(first, second):
    return jnp.sum(first * second, axis=(1, 2, 3))


def shards(macro_adjoint, slip_code, grain_id, grain_modulus, slip_softening, rve_spot):
    rve_count = slip_code.shape[0]
    cells = slip_code.shape[2]
    spot_count = macro_adjoint.shape[0] * lax.axis_size("hot")
    column = jnp.arange(cells) % RES
    upper_mask = (column != RES - 1).astype(jnp.float32)
    lower_mask = (column != 0).astype(jnp.float32)
    table = jnp.concatenate([grain_modulus[None, :], slip_softening.T], 0)

    def stiff_one(inputs):
        codes, grain_cells = inputs
        flat_codes = codes.reshape(-1)
        flat_grains = grain_cells.reshape(-1)
        onehot = (jnp.arange(GRAINS)[:, None] == flat_grains[None, :]).astype(jnp.float32)
        looked = jnp.dot(
            table, onehot, precision=lax.Precision.HIGHEST, preferred_element_type=jnp.float32
        )
        softening = jnp.zeros(flat_codes.shape, jnp.float32)
        for slip in range(SLIPS):
            active = (flat_codes // 2**slip % 2).astype(jnp.float32)
            softening = softening + active * looked[1 + slip]
        return (looked[0] / (1.0 + softening)).reshape(codes.shape)

    spot_onehot = (rve_spot[:, None] == jnp.arange(spot_count)[None, :]).astype(jnp.float32)
    parts, hot_me = axis_gather(macro_adjoint, "hot")
    if hot_me is None:
        all_strains = parts[0]
    else:
        local = macro_adjoint.shape[0]
        ordered = []
        for j in range(len(parts)):
            pick = [(hot_me ^ o) == j for o in range(len(parts))]
            block = parts[0]
            for o in range(1, len(parts)):
                block = jnp.where(pick[o], parts[o], block)
            ordered.append(block)
        all_strains = jnp.concatenate(ordered, 0)
    strains = jnp.dot(
        spot_onehot,
        all_strains,
        precision=lax.Precision.HIGHEST,
        preferred_element_type=jnp.float32,
    )
    stiff_slabs = stiffness(table, slip_code, grain_id)
    stiff = lax.all_to_all(stiff_slabs, "xc", 0, 1, tiled=True)
    mine = lax.axis_index("xc")
    strains = lax.dynamic_slice_in_dim(strains, mine, 1, 0)
    padded = padded_2(stiff, (("yb", 1),), 2)
    wide = padded[:, 1:-1]
    wide_xup, wide_xdn = padded[:, 2:], padded[:, :-2]
    wide_yup, wide_ydn = shift_cells(wide, RES), shift_cells(wide, -RES)
    wide_zup, wide_zdn = shift_cells(wide, 1) * upper_mask, shift_cells(wide, -1) * lower_mask

    def inner(planes):
        return planes[:, 1:-1]

    near_xup, near_xdn = inner(wide_xup), inner(wide_xdn)
    near_yup, near_ydn = inner(wide_yup), inner(wide_ydn)
    near_zup, near_zdn = inner(wide_zup), inner(wide_zdn)
    face_xup = 0.5 * (stiff + near_xup)
    face_xdn = 0.5 * (stiff + near_xdn)
    face_yup = 0.5 * (stiff + near_yup)
    face_ydn = 0.5 * (stiff + near_ydn)
    face_zup = 0.5 * (stiff + near_zup)
    face_zdn = 0.5 * (stiff + near_zdn)
    diagonal_sum = (mass_term + face_xup + face_xdn + face_yup + face_ydn + face_zup + face_zdn)[
        :, None
    ]
    wide_gradients = [
        0.5 * (wide_xup - wide_xdn),
        0.5 * (wide_yup - wide_ydn),
        0.5 * (wide_zup - wide_zdn),
    ]
    gradients = [inner(g) for g in wide_gradients]
    tensor = [
        [strains[:, 0], strains[:, 5], strains[:, 4]],
        [strains[:, 5], strains[:, 1], strains[:, 3]],
        [strains[:, 4], strains[:, 3], strains[:, 2]],
    ]
    wide_source = jnp.stack(
        [
            wide_gradients[0] * tensor[comp][0][:, None, None]
            + wide_gradients[1] * tensor[comp][1][:, None, None]
            + wide_gradients[2] * tensor[comp][2][:, None, None]
            for comp in range(3)
        ],
        1,
    )
    source = wide_source[:, :, 1:-1]
    plane_block = lax.axis_index("yb")
    source_edges = jnp.concatenate(
        [
            jnp.where(plane_block != 0, wide_source[:, :, :1], 0.0),
            jnp.where(plane_block != lax.axis_size("yb") - 1, wide_source[:, :, -1:], 0.0),
        ],
        2,
    )

    def expand(values):
        return values[:, None, None, None]

    def boundary_planes(value):
        size = lax.axis_size("yb")
        up = [(i, i + 1) for i in range(size - 1)]
        down = [(i + 1, i) for i in range(size - 1)]
        before = lax.ppermute(value[:, :, -1:], "yb", up)
        after = lax.ppermute(value[:, :, :1], "yb", down)
        return jnp.concatenate([before, after], 2)

    def operate(direction, edges):
        wide = jnp.concatenate([edges[:, :, :1], direction, edges[:, :, 1:]], 2)
        return (
            diagonal_sum * direction
            - face_xup[:, None] * wide[:, :, 2:]
            - face_xdn[:, None] * wide[:, :, :-2]
            - face_yup[:, None] * shift_cells(direction, RES)
            - face_ydn[:, None] * shift_cells(direction, -RES)
            - face_zup[:, None] * (shift_cells(direction, 1) * upper_mask)
            - face_zdn[:, None] * (shift_cells(direction, -1) * lower_mask)
        )

    answer = jnp.zeros_like(source)
    residual = source
    direction = source
    residual_edges = source_edges
    direction_edges = residual_edges
    for step in range(ITERS):
        image = operate(direction, direction_edges)
        last = step + 1 == ITERS
        if not last:
            image_edges = boundary_planes(image)
        terms = [
            local_dot(direction, image),
            local_dot(residual, residual),
            local_dot(residual, image),
            local_dot(image, image),
        ]
        if last:
            for held in (answer, direction):
                terms += [
                    jnp.sum(held[:, comp] * gradients[other], axis=(1, 2))
                    for comp in range(3)
                    for other in range(3)
                ]
            terms.append(jnp.sum(stiff, axis=(1, 2)))
        local = jnp.stack(terms, -1)
        if last:
            sums = axis_sum(local, "yb")
            norm_now = sums[:, 1]
            alpha = norm_now / sums[:, 0]
        else:
            lanes = axis_sum(jnp.broadcast_to(local[:, :, None], local.shape + (128,)), "yb")
            lane_alpha = lanes[:, 1] / lanes[:, 0]
            lane_next = lanes[:, 1] - 2.0 * lane_alpha * lanes[:, 2] + lane_alpha * lane_alpha * lanes[:, 3]
            lane_beta = lane_next / lanes[:, 1]
            alpha = lane_alpha[:, 0]
        answer = answer + expand(alpha) * direction
        if last:
            break
        beta = expand(lane_beta[:, 0])
        residual = residual - expand(alpha) * image
        residual_edges = residual_edges - expand(alpha) * image_edges
        direction = residual + beta * direction
        direction_edges = residual_edges + beta * direction_edges
    volume = float(RES**3)
    moments = sums[:, 4:13] + alpha[:, None] * sums[:, 13:22]
    pair_sum = jnp.take(moments, jnp.array([0, 4, 8, 5, 2, 1]), axis=1) + jnp.take(
        moments, jnp.array([0, 4, 8, 7, 6, 3]), axis=1
    )
    rve_one = sums[:, 22:23] / volume * strains - 0.5 * pair_sum / volume
    per_spot = float(rve_count * lax.axis_size("hot") // spot_count)
    placed = (jnp.arange(rve_count)[:, None] == mine).astype(jnp.float32) * rve_one
    rve_totals = axis_sum(placed, "xc")
    spot_local = jnp.dot(
        spot_onehot.T,
        rve_totals,
        precision=lax.Precision.HIGHEST,
        preferred_element_type=jnp.float32,
    )
    owned = axis_reduce_scatter(spot_local, "hot")
    return (owned / per_spot, lax.all_to_all(answer, "xc", 2, 0, tiled=True))


def solution(mesh):
    hot, dom = mesh.shape["hot"], mesh.shape["dom"]
    rves_here = RVES // hot
    grouped = Mesh(mesh.devices.reshape(hot, dom // rves_here, rves_here), ("hot", "yb", "xc"))
    return jax.shard_map(
        shards,
        mesh=grouped,
        in_specs=(
            P("hot", None),
            P("hot", ("yb", "xc"), None),
            P("hot", ("yb", "xc"), None),
            P(),
            P(),
            P("hot"),
        ),
        out_specs=(P("hot", None), P("hot", None, ("yb", "xc"), None)),
        check_vma=False,
    )
```

```python
import jax
import jax.numpy as jnp
from jax import lax
from jax.experimental import pallas as pl
from jax.sharding import Mesh, PartitionSpec as P

RES = 64
SLIPS = 12
GRAINS = 64
ITERS = 8
RVES = 32


mass_term = 0.02


def padded_2(value, sides, width):
    for axis, dim in sides:
        devices, length = (lax.axis_size(axis), value.shape[dim])
        up = [(i, (i + 1) % devices) for i in range(devices - 1)]
        down = [(j, i) for i, j in up]
        last = lax.slice_in_dim(value, length - width, length, axis=dim)
        leading = lax.slice_in_dim(value, 0, width, axis=dim)
        before = lax.ppermute(last, axis, up)
        after = lax.ppermute(leading, axis, down)
        value = jnp.concatenate([before, value, after], axis=dim)
    return value


def xor_groups(size):
    bits = size.bit_length() - 1
    if size != 1 << bits:
        return None
    groups = [(0, 1)] if bits % 2 else []
    lo = bits % 2
    while lo < bits:
        groups.append((lo, 2))
        lo += 2
    return groups


def tree_sum(vals, nb):
    cur = dict(vals)
    for level in range(nb):
        cur = {o: v + cur[o | (1 << level)] for o, v in cur.items() if not o & (1 << level)}
    return cur[0]


def axis_sum(value, axis):
    size = lax.axis_size(axis)
    groups = xor_groups(size)
    if groups is None:
        return lax.psum(value, axis)
    for lo, nb in groups:
        vals = {0: value}
        for o in range(1, 1 << nb):
            mask = o << lo
            vals[o] = lax.ppermute(value, axis, [(i, i ^ mask) for i in range(size)])
        value = tree_sum(vals, nb)
    return value


def axis_gather(value, axis):
    size = lax.axis_size(axis)
    if xor_groups(size) is None:
        return [lax.all_gather(value, axis, axis=0, tiled=True)], None
    parts = [value] + [
        lax.ppermute(value, axis, [(i, i ^ o) for i in range(size)]) for o in range(1, size)
    ]
    return parts, lax.axis_index(axis)


def axis_reduce_scatter(value, axis):
    size = lax.axis_size(axis)
    if xor_groups(size) is None:
        return lax.psum_scatter(value, axis, scatter_dimension=0, tiled=True)
    me = lax.axis_index(axis)
    block = value.shape[0] // size
    nb = size.bit_length() - 1
    vals = {0: lax.dynamic_slice_in_dim(value, me * block, block, 0)}
    for o in range(1, size):
        wanted = lax.dynamic_slice_in_dim(value, (me ^ o) * block, block, 0)
        vals[o] = lax.ppermute(wanted, axis, [(i, i ^ o) for i in range(size)])
    return tree_sum(vals, nb)


CHUNK = 512


def stiffness_kernel(pieces_ref, codes_ref, grains_ref, out_ref):
    rows = pieces_ref.shape[1]

    def chunk(c, carry):
        at = pl.multiple_of(c * CHUNK, CHUNK)
        for plane in range(codes_ref.shape[1]):
            grains = grains_ref[0, plane : plane + 1, pl.ds(at, CHUNK)]
            codes = codes_ref[0, plane : plane + 1, pl.ds(at, CHUNK)]
            onehot = (lax.broadcasted_iota(jnp.int32, (GRAINS, CHUNK), 0) == grains).astype(jnp.bfloat16)
            looked = jnp.dot(pieces_ref[0], onehot, preferred_element_type=jnp.float32)
            looked = looked + jnp.dot(pieces_ref[1], onehot, preferred_element_type=jnp.float32)
            looked = looked + jnp.dot(pieces_ref[2], onehot, preferred_element_type=jnp.float32)
            softening = jnp.zeros((1, CHUNK), jnp.float32)
            for slip in range(SLIPS):
                active = ((codes >> slip) & 1).astype(jnp.float32)
                softening = softening + active * looked[1 + slip : 2 + slip, :]
            out_ref[0, plane : plane + 1, pl.ds(at, CHUNK)] = looked[0:1, :] / (1.0 + softening)
        return carry

    lax.fori_loop(0, codes_ref.shape[2] // CHUNK, chunk, 0)
    del rows


def stiffness(table, slip_code, grain_id):
    high = lax.reduce_precision(table, exponent_bits=8, mantissa_bits=7)
    rest = table - high
    middle = lax.reduce_precision(rest, exponent_bits=8, mantissa_bits=7)
    low = rest - middle
    pieces = jnp.stack([high, middle, low]).astype(jnp.bfloat16)
    pieces = jnp.pad(pieces, ((0, 0), (0, 16 - table.shape[0]), (0, 0)))
    rves, planes, cells = slip_code.shape
    block = pl.BlockSpec((1, planes, cells), lambda r: (r, 0, 0))
    return pl.pallas_call(
        stiffness_kernel,
        grid=(rves,),
        in_specs=[pl.BlockSpec(pieces.shape, lambda r: (0, 0, 0)), block, block],
        out_specs=block,
        out_shape=jax.ShapeDtypeStruct(slip_code.shape, jnp.float32),
    )(pieces, slip_code, grain_id)


def shift_cells(field, step):
    filler = jnp.zeros(field.shape[:-1] + (abs(step),), field.dtype)
    if step > 0:
        return jnp.concatenate([field[..., step:], filler], -1)
    return jnp.concatenate([filler, field[..., :step]], -1)


def local_dot(first, second):
    return jnp.sum(first * second, axis=(1, 2, 3))


def shards(macro_adjoint, slip_code, grain_id, grain_modulus, slip_softening, rve_spot):
    rve_count = slip_code.shape[0]
    cells = slip_code.shape[2]
    spot_count = macro_adjoint.shape[0] * lax.axis_size("hot")
    column = jnp.arange(cells) % RES
    upper_mask = (column != RES - 1).astype(jnp.float32)
    lower_mask = (column != 0).astype(jnp.float32)
    table = jnp.concatenate([grain_modulus[None, :], slip_softening.T], 0)

    def stiff_one(inputs):
        codes, grain_cells = inputs
        flat_codes = codes.reshape(-1)
        flat_grains = grain_cells.reshape(-1)
        onehot = (jnp.arange(GRAINS)[:, None] == flat_grains[None, :]).astype(jnp.float32)
        looked = jnp.dot(
            table, onehot, precision=lax.Precision.HIGHEST, preferred_element_type=jnp.float32
        )
        softening = jnp.zeros(flat_codes.shape, jnp.float32)
        for slip in range(SLIPS):
            active = (flat_codes // 2**slip % 2).astype(jnp.float32)
            softening = softening + active * looked[1 + slip]
        return (looked[0] / (1.0 + softening)).reshape(codes.shape)

    spot_onehot = (rve_spot[:, None] == jnp.arange(spot_count)[None, :]).astype(jnp.float32)
    parts, hot_me = axis_gather(macro_adjoint, "hot")
    if hot_me is None:
        all_strains = parts[0]
    else:
        local = macro_adjoint.shape[0]
        ordered = []
        for j in range(len(parts)):
            pick = [(hot_me ^ o) == j for o in range(len(parts))]
            block = parts[0]
            for o in range(1, len(parts)):
                block = jnp.where(pick[o], parts[o], block)
            ordered.append(block)
        all_strains = jnp.concatenate(ordered, 0)
    strains = jnp.dot(
        spot_onehot,
        all_strains,
        precision=lax.Precision.HIGHEST,
        preferred_element_type=jnp.float32,
    )
    stiff_slabs = stiffness(table, slip_code, grain_id)
    stiff = lax.all_to_all(stiff_slabs, "xc", 0, 1, tiled=True)
    mine = lax.axis_index("xc")
    strains = lax.dynamic_slice_in_dim(strains, mine, 1, 0)
    margin = ITERS
    planes = stiff.shape[1]
    padded = padded_2(stiff, (("yb", 1),), margin + 1)
    wide = padded[:, 1:-1]
    wide_xup, wide_xdn = padded[:, 2:], padded[:, :-2]
    wide_yup, wide_ydn = shift_cells(wide, RES), shift_cells(wide, -RES)
    wide_zup, wide_zdn = shift_cells(wide, 1) * upper_mask, shift_cells(wide, -1) * lower_mask
    wide_faces = [0.5 * (wide + near) for near in (wide_xup, wide_xdn, wide_yup, wide_ydn, wide_zup, wide_zdn)]
    wide_diagonal = mass_term + wide_faces[0] + wide_faces[1] + wide_faces[2] + wide_faces[3] + wide_faces[4] + wide_faces[5]
    wide_gradients = [
        0.5 * (wide_xup - wide_xdn),
        0.5 * (wide_yup - wide_ydn),
        0.5 * (wide_zup - wide_zdn),
    ]
    plane_at = planes * lax.axis_index("yb") - margin + jnp.arange(planes + 2 * margin)
    inside = ((plane_at >= 0) & (plane_at < planes * lax.axis_size("yb")))[None, None, :, None]

    def within(values, keep, axis=1):
        cut = margin - keep
        return lax.slice_in_dim(values, cut, values.shape[axis] - cut, axis=axis)

    gradients = [within(g, 0) for g in wide_gradients]
    tensor = [
        [strains[:, 0], strains[:, 5], strains[:, 4]],
        [strains[:, 5], strains[:, 1], strains[:, 3]],
        [strains[:, 4], strains[:, 3], strains[:, 2]],
    ]
    wide_source = jnp.stack(
        [
            wide_gradients[0] * tensor[comp][0][:, None, None]
            + wide_gradients[1] * tensor[comp][1][:, None, None]
            + wide_gradients[2] * tensor[comp][2][:, None, None]
            for comp in range(3)
        ],
        1,
    )
    wide_source = jnp.where(inside, wide_source, 0.0)

    def expand(values):
        return values[:, None, None, None]

    def operate(direction, keep):
        centre = direction[:, :, 1:-1]
        faces = [within(f, keep)[:, None] for f in wide_faces]
        return (
            within(wide_diagonal, keep)[:, None] * centre
            - faces[0] * direction[:, :, 2:]
            - faces[1] * direction[:, :, :-2]
            - faces[2] * shift_cells(centre, RES)
            - faces[3] * shift_cells(centre, -RES)
            - faces[4] * (shift_cells(centre, 1) * upper_mask)
            - faces[5] * (shift_cells(centre, -1) * lower_mask)
        )

    def middle(values, held):
        return lax.slice_in_dim(values, held, values.shape[2] - held, axis=2)

    residual = wide_source
    direction = wide_source
    answer = jnp.zeros_like(middle(wide_source, margin))
    for step in range(ITERS):
        held = margin - step
        image = operate(direction, held - 1)
        last = step + 1 == ITERS
        inner_direction = middle(direction, held)
        inner_residual = middle(residual, held)
        inner_image = middle(image, held - 1)
        terms = [
            local_dot(inner_direction, inner_image),
            local_dot(inner_residual, inner_residual),
            local_dot(inner_residual, inner_image),
            local_dot(inner_image, inner_image),
        ]
        if last:
            for value in (answer, inner_direction):
                terms += [
                    jnp.sum(value[:, comp] * gradients[other], axis=(1, 2))
                    for comp in range(3)
                    for other in range(3)
                ]
            terms.append(jnp.sum(stiff, axis=(1, 2)))
        local = jnp.stack(terms, -1)
        if last:
            sums = axis_sum(local, "yb")
            norm_now = sums[:, 1]
            alpha = norm_now / sums[:, 0]
        else:
            lanes = axis_sum(jnp.broadcast_to(local[:, :, None], local.shape + (128,)), "yb")
            lane_alpha = lanes[:, 1] / lanes[:, 0]
            lane_next = lanes[:, 1] - 2.0 * lane_alpha * lanes[:, 2] + lane_alpha * lane_alpha * lanes[:, 3]
            lane_beta = lane_next / lanes[:, 1]
            alpha = lane_alpha[:, 0]
        answer = answer + expand(alpha) * inner_direction
        if last:
            break
        beta = expand(lane_beta[:, 0])
        keep_inside = within(inside, held - 1, axis=2)
        residual = jnp.where(keep_inside, middle(residual, 1) - expand(alpha) * image, 0.0)
        direction = jnp.where(keep_inside, residual + beta * middle(direction, 1), 0.0)
    volume = float(RES**3)
    moments = sums[:, 4:13] + alpha[:, None] * sums[:, 13:22]
    pair_sum = jnp.take(moments, jnp.array([0, 4, 8, 5, 2, 1]), axis=1) + jnp.take(
        moments, jnp.array([0, 4, 8, 7, 6, 3]), axis=1
    )
    rve_one = sums[:, 22:23] / volume * strains - 0.5 * pair_sum / volume
    per_spot = float(rve_count * lax.axis_size("hot") // spot_count)
    placed = (jnp.arange(rve_count)[:, None] == mine).astype(jnp.float32) * rve_one
    rve_totals = axis_sum(placed, "xc")
    spot_local = jnp.dot(
        spot_onehot.T,
        rve_totals,
        precision=lax.Precision.HIGHEST,
        preferred_element_type=jnp.float32,
    )
    owned = axis_reduce_scatter(spot_local, "hot")
    return (owned / per_spot, lax.all_to_all(answer, "xc", 2, 0, tiled=True))


def solution(mesh):
    hot, dom = mesh.shape["hot"], mesh.shape["dom"]
    rves_here = RVES // hot
    grouped = Mesh(mesh.devices.reshape(hot, dom // rves_here, rves_here), ("hot", "yb", "xc"))
    return jax.shard_map(
        shards,
        mesh=grouped,
        in_specs=(
            P("hot", None),
            P("hot", ("yb", "xc"), None),
            P("hot", ("yb", "xc"), None),
            P(),
            P(),
            P("hot"),
        ),
        out_specs=(P("hot", None), P("hot", None, ("yb", "xc"), None)),
        check_vma=False,
    )
```

```python
import jax
import jax.numpy as jnp
from jax import lax
from jax.experimental import pallas as pl
from jax.sharding import Mesh, PartitionSpec as P

RES = 64
SLIPS = 12
GRAINS = 64
ITERS = 8
RVES = 32


mass_term = 0.02


def padded_2(value, sides, width):
    for axis, dim in sides:
        devices, length = (lax.axis_size(axis), value.shape[dim])
        up = [(i, (i + 1) % devices) for i in range(devices - 1)]
        down = [(j, i) for i, j in up]
        last = lax.slice_in_dim(value, length - width, length, axis=dim)
        leading = lax.slice_in_dim(value, 0, width, axis=dim)
        before = lax.ppermute(last, axis, up)
        after = lax.ppermute(leading, axis, down)
        value = jnp.concatenate([before, value, after], axis=dim)
    return value


def xor_groups(size):
    bits = size.bit_length() - 1
    if size != 1 << bits:
        return None
    groups = [(0, 1)] if bits % 2 else []
    lo = bits % 2
    while lo < bits:
        groups.append((lo, 2))
        lo += 2
    return groups


def tree_sum(vals, nb):
    cur = dict(vals)
    for level in range(nb):
        cur = {o: v + cur[o | (1 << level)] for o, v in cur.items() if not o & (1 << level)}
    return cur[0]


def axis_sum(value, axis):
    size = lax.axis_size(axis)
    groups = xor_groups(size)
    if groups is None:
        return lax.psum(value, axis)
    for lo, nb in groups:
        vals = {0: value}
        for o in range(1, 1 << nb):
            mask = o << lo
            vals[o] = lax.ppermute(value, axis, [(i, i ^ mask) for i in range(size)])
        value = tree_sum(vals, nb)
    return value


def axis_gather(value, axis):
    size = lax.axis_size(axis)
    if xor_groups(size) is None:
        return [lax.all_gather(value, axis, axis=0, tiled=True)], None
    parts = [value] + [
        lax.ppermute(value, axis, [(i, i ^ o) for i in range(size)]) for o in range(1, size)
    ]
    return parts, lax.axis_index(axis)


def axis_reduce_scatter(value, axis):
    size = lax.axis_size(axis)
    if xor_groups(size) is None:
        return lax.psum_scatter(value, axis, scatter_dimension=0, tiled=True)
    me = lax.axis_index(axis)
    block = value.shape[0] // size
    nb = size.bit_length() - 1
    vals = {0: lax.dynamic_slice_in_dim(value, me * block, block, 0)}
    for o in range(1, size):
        wanted = lax.dynamic_slice_in_dim(value, (me ^ o) * block, block, 0)
        vals[o] = lax.ppermute(wanted, axis, [(i, i ^ o) for i in range(size)])
    return tree_sum(vals, nb)


CHUNK = 512


def stiffness_kernel(pieces_ref, codes_ref, grains_ref, out_ref):
    rows = pieces_ref.shape[1]

    def chunk(c, carry):
        at = pl.multiple_of(c * CHUNK, CHUNK)
        for plane in range(codes_ref.shape[1]):
            grains = grains_ref[0, plane : plane + 1, pl.ds(at, CHUNK)]
            codes = codes_ref[0, plane : plane + 1, pl.ds(at, CHUNK)]
            onehot = (lax.broadcasted_iota(jnp.int32, (GRAINS, CHUNK), 0) == grains).astype(jnp.bfloat16)
            looked = jnp.dot(pieces_ref[0], onehot, preferred_element_type=jnp.float32)
            looked = looked + jnp.dot(pieces_ref[1], onehot, preferred_element_type=jnp.float32)
            looked = looked + jnp.dot(pieces_ref[2], onehot, preferred_element_type=jnp.float32)
            softening = jnp.zeros((1, CHUNK), jnp.float32)
            for slip in range(SLIPS):
                active = ((codes >> slip) & 1).astype(jnp.float32)
                softening = softening + active * looked[1 + slip : 2 + slip, :]
            out_ref[0, plane : plane + 1, pl.ds(at, CHUNK)] = looked[0:1, :] / (1.0 + softening)
        return carry

    lax.fori_loop(0, codes_ref.shape[2] // CHUNK, chunk, 0)
    del rows


def stiffness(table, slip_code, grain_id):
    high = lax.reduce_precision(table, exponent_bits=8, mantissa_bits=7)
    rest = table - high
    middle = lax.reduce_precision(rest, exponent_bits=8, mantissa_bits=7)
    low = rest - middle
    pieces = jnp.stack([high, middle, low]).astype(jnp.bfloat16)
    pieces = jnp.pad(pieces, ((0, 0), (0, 16 - table.shape[0]), (0, 0)))
    rves, planes, cells = slip_code.shape
    block = pl.BlockSpec((1, planes, cells), lambda r: (r, 0, 0))
    return pl.pallas_call(
        stiffness_kernel,
        grid=(rves,),
        in_specs=[pl.BlockSpec(pieces.shape, lambda r: (0, 0, 0)), block, block],
        out_specs=block,
        out_shape=jax.ShapeDtypeStruct(slip_code.shape, jnp.float32),
    )(pieces, slip_code, grain_id)


def shift_cells(field, step):
    filler = jnp.zeros(field.shape[:-1] + (abs(step),), field.dtype)
    if step > 0:
        return jnp.concatenate([field[..., step:], filler], -1)
    return jnp.concatenate([filler, field[..., :step]], -1)


def local_dot(first, second):
    return jnp.sum(first * second, axis=(1, 2, 3))


def shards(macro_adjoint, slip_code, grain_id, grain_modulus, slip_softening, rve_spot):
    rve_count = slip_code.shape[0]
    cells = slip_code.shape[2]
    spot_count = macro_adjoint.shape[0] * lax.axis_size("hot")
    column = jnp.arange(cells) % RES
    upper_mask = (column != RES - 1).astype(jnp.float32)
    lower_mask = (column != 0).astype(jnp.float32)
    table = jnp.concatenate([grain_modulus[None, :], slip_softening.T], 0)

    def stiff_one(inputs):
        codes, grain_cells = inputs
        flat_codes = codes.reshape(-1)
        flat_grains = grain_cells.reshape(-1)
        onehot = (jnp.arange(GRAINS)[:, None] == flat_grains[None, :]).astype(jnp.float32)
        looked = jnp.dot(
            table, onehot, precision=lax.Precision.HIGHEST, preferred_element_type=jnp.float32
        )
        softening = jnp.zeros(flat_codes.shape, jnp.float32)
        for slip in range(SLIPS):
            active = (flat_codes // 2**slip % 2).astype(jnp.float32)
            softening = softening + active * looked[1 + slip]
        return (looked[0] / (1.0 + softening)).reshape(codes.shape)

    spot_onehot = (rve_spot[:, None] == jnp.arange(spot_count)[None, :]).astype(jnp.float32)
    parts, hot_me = axis_gather(macro_adjoint, "hot")
    if hot_me is None:
        all_strains = parts[0]
    else:
        local = macro_adjoint.shape[0]
        ordered = []
        for j in range(len(parts)):
            pick = [(hot_me ^ o) == j for o in range(len(parts))]
            block = parts[0]
            for o in range(1, len(parts)):
                block = jnp.where(pick[o], parts[o], block)
            ordered.append(block)
        all_strains = jnp.concatenate(ordered, 0)
    strains = jnp.dot(
        spot_onehot,
        all_strains,
        precision=lax.Precision.HIGHEST,
        preferred_element_type=jnp.float32,
    )
    stiff_slabs = stiffness(table, slip_code, grain_id)
    stiff = lax.all_to_all(stiff_slabs, "xc", 0, 1, tiled=True)
    mine = lax.axis_index("xc")
    strains = lax.dynamic_slice_in_dim(strains, mine, 1, 0)
    margin = ITERS
    planes = stiff.shape[1]
    padded = padded_2(stiff, (("yb", 1),), margin + 1)
    wide = padded[:, 1:-1]
    wide_xup, wide_xdn = padded[:, 2:], padded[:, :-2]
    wide_yup, wide_ydn = shift_cells(wide, RES), shift_cells(wide, -RES)
    wide_zup, wide_zdn = shift_cells(wide, 1) * upper_mask, shift_cells(wide, -1) * lower_mask
    wide_gradients = [
        0.5 * (wide_xup - wide_xdn),
        0.5 * (wide_yup - wide_ydn),
        0.5 * (wide_zup - wide_zdn),
    ]
    plane_at = planes * lax.axis_index("yb") - margin + jnp.arange(planes + 2 * margin)
    inside = ((plane_at >= 0) & (plane_at < planes * lax.axis_size("yb")))[None, None, :, None]

    def within(values, keep, axis=1):
        cut = margin - keep
        return lax.slice_in_dim(values, cut, values.shape[axis] - cut, axis=axis)

    gradients = [within(g, 0) for g in wide_gradients]
    tensor = [
        [strains[:, 0], strains[:, 5], strains[:, 4]],
        [strains[:, 5], strains[:, 1], strains[:, 3]],
        [strains[:, 4], strains[:, 3], strains[:, 2]],
    ]
    wide_source = jnp.stack(
        [
            wide_gradients[0] * tensor[comp][0][:, None, None]
            + wide_gradients[1] * tensor[comp][1][:, None, None]
            + wide_gradients[2] * tensor[comp][2][:, None, None]
            for comp in range(3)
        ],
        1,
    )
    wide_source = jnp.where(inside, wide_source, 0.0)

    def expand(values):
        return values[:, None, None, None]

    def operate(direction, keep):
        centre = direction[:, :, 1:-1]
        here = within(wide, keep)
        faces = [
            0.5 * (here + within(near, keep))
            for near in (wide_xup, wide_xdn, wide_yup, wide_ydn, wide_zup, wide_zdn)
        ]
        diagonal = mass_term + faces[0] + faces[1] + faces[2] + faces[3] + faces[4] + faces[5]
        faces = [f[:, None] for f in faces]
        return (
            diagonal[:, None] * centre
            - faces[0] * direction[:, :, 2:]
            - faces[1] * direction[:, :, :-2]
            - faces[2] * shift_cells(centre, RES)
            - faces[3] * shift_cells(centre, -RES)
            - faces[4] * (shift_cells(centre, 1) * upper_mask)
            - faces[5] * (shift_cells(centre, -1) * lower_mask)
        )

    def middle(values, held):
        return lax.slice_in_dim(values, held, values.shape[2] - held, axis=2)

    residual = wide_source
    direction = wide_source
    answer = jnp.zeros_like(middle(wide_source, margin))
    for step in range(ITERS):
        held = margin - step
        image = operate(direction, held - 1)
        last = step + 1 == ITERS
        inner_direction = middle(direction, held)
        inner_residual = middle(residual, held)
        inner_image = middle(image, held - 1)
        terms = [
            local_dot(inner_direction, inner_image),
            local_dot(inner_residual, inner_residual),
            local_dot(inner_residual, inner_image),
            local_dot(inner_image, inner_image),
        ]
        if last:
            for value in (answer, inner_direction):
                terms += [
                    jnp.sum(value[:, comp] * gradients[other], axis=(1, 2))
                    for comp in range(3)
                    for other in range(3)
                ]
            terms.append(jnp.sum(stiff, axis=(1, 2)))
        local = jnp.stack(terms, -1)
        if last:
            sums = axis_sum(local, "yb")
            norm_now = sums[:, 1]
            alpha = norm_now / sums[:, 0]
        else:
            lanes = axis_sum(jnp.broadcast_to(local[:, :, None], local.shape + (128,)), "yb")
            lane_alpha = lanes[:, 1] / lanes[:, 0]
            lane_next = lanes[:, 1] - 2.0 * lane_alpha * lanes[:, 2] + lane_alpha * lane_alpha * lanes[:, 3]
            lane_beta = lane_next / lanes[:, 1]
            alpha = lane_alpha[:, 0]
        answer = answer + expand(alpha) * inner_direction
        if last:
            break
        beta = expand(lane_beta[:, 0])
        keep_inside = within(inside, held - 1, axis=2)
        residual = jnp.where(keep_inside, middle(residual, 1) - expand(alpha) * image, 0.0)
        direction = jnp.where(keep_inside, residual + beta * middle(direction, 1), 0.0)
    volume = float(RES**3)
    moments = sums[:, 4:13] + alpha[:, None] * sums[:, 13:22]
    pair_sum = jnp.take(moments, jnp.array([0, 4, 8, 5, 2, 1]), axis=1) + jnp.take(
        moments, jnp.array([0, 4, 8, 7, 6, 3]), axis=1
    )
    rve_one = sums[:, 22:23] / volume * strains - 0.5 * pair_sum / volume
    per_spot = float(rve_count * lax.axis_size("hot") // spot_count)
    placed = (jnp.arange(rve_count)[:, None] == mine).astype(jnp.float32) * rve_one
    rve_totals = axis_sum(placed, "xc")
    spot_local = jnp.dot(
        spot_onehot.T,
        rve_totals,
        precision=lax.Precision.HIGHEST,
        preferred_element_type=jnp.float32,
    )
    owned = axis_reduce_scatter(spot_local, "hot")
    return (owned / per_spot, lax.all_to_all(answer, "xc", 2, 0, tiled=True))


def solution(mesh):
    hot, dom = mesh.shape["hot"], mesh.shape["dom"]
    rves_here = RVES // hot
    grouped = Mesh(mesh.devices.reshape(hot, dom // rves_here, rves_here), ("hot", "yb", "xc"))
    return jax.shard_map(
        shards,
        mesh=grouped,
        in_specs=(
            P("hot", None),
            P("hot", ("yb", "xc"), None),
            P("hot", ("yb", "xc"), None),
            P(),
            P(),
            P("hot"),
        ),
        out_specs=(P("hot", None), P("hot", None, ("yb", "xc"), None)),
        check_vma=False,
    )
```

```python
import jax
import jax.numpy as jnp
from jax import lax
from jax.experimental import pallas as pl
from jax.sharding import Mesh, PartitionSpec as P

RES = 64
SLIPS = 12
GRAINS = 64
ITERS = 8
RVES = 32


mass_term = 0.02


def padded_2(value, sides, width):
    for axis, dim in sides:
        devices, length = (lax.axis_size(axis), value.shape[dim])
        up = [(i, (i + 1) % devices) for i in range(devices - 1)]
        down = [(j, i) for i, j in up]
        last = lax.slice_in_dim(value, length - width, length, axis=dim)
        leading = lax.slice_in_dim(value, 0, width, axis=dim)
        before = lax.ppermute(last, axis, up)
        after = lax.ppermute(leading, axis, down)
        value = jnp.concatenate([before, value, after], axis=dim)
    return value


def xor_groups(size):
    bits = size.bit_length() - 1
    if size != 1 << bits:
        return None
    groups = [(0, 1)] if bits % 2 else []
    lo = bits % 2
    while lo < bits:
        groups.append((lo, 2))
        lo += 2
    return groups


def tree_sum(vals, nb):
    cur = dict(vals)
    for level in range(nb):
        cur = {o: v + cur[o | (1 << level)] for o, v in cur.items() if not o & (1 << level)}
    return cur[0]


def axis_sum(value, axis):
    size = lax.axis_size(axis)
    groups = xor_groups(size)
    if groups is None:
        return lax.psum(value, axis)
    for lo, nb in groups:
        vals = {0: value}
        for o in range(1, 1 << nb):
            mask = o << lo
            vals[o] = lax.ppermute(value, axis, [(i, i ^ mask) for i in range(size)])
        value = tree_sum(vals, nb)
    return value


def axis_gather(value, axis):
    size = lax.axis_size(axis)
    if xor_groups(size) is None:
        return [lax.all_gather(value, axis, axis=0, tiled=True)], None
    parts = [value] + [
        lax.ppermute(value, axis, [(i, i ^ o) for i in range(size)]) for o in range(1, size)
    ]
    return parts, lax.axis_index(axis)


def axis_reduce_scatter(value, axis):
    size = lax.axis_size(axis)
    if xor_groups(size) is None:
        return lax.psum_scatter(value, axis, scatter_dimension=0, tiled=True)
    me = lax.axis_index(axis)
    block = value.shape[0] // size
    nb = size.bit_length() - 1
    vals = {0: lax.dynamic_slice_in_dim(value, me * block, block, 0)}
    for o in range(1, size):
        wanted = lax.dynamic_slice_in_dim(value, (me ^ o) * block, block, 0)
        vals[o] = lax.ppermute(wanted, axis, [(i, i ^ o) for i in range(size)])
    return tree_sum(vals, nb)


CHUNK = 512


def stiffness_kernel(pieces_ref, codes_ref, grains_ref, out_ref):
    rows = pieces_ref.shape[1]

    def chunk(c, carry):
        at = pl.multiple_of(c * CHUNK, CHUNK)
        for plane in range(codes_ref.shape[1]):
            grains = grains_ref[0, plane : plane + 1, pl.ds(at, CHUNK)]
            codes = codes_ref[0, plane : plane + 1, pl.ds(at, CHUNK)]
            onehot = (lax.broadcasted_iota(jnp.int32, (GRAINS, CHUNK), 0) == grains).astype(jnp.bfloat16)
            looked = jnp.dot(pieces_ref[0], onehot, preferred_element_type=jnp.float32)
            looked = looked + jnp.dot(pieces_ref[1], onehot, preferred_element_type=jnp.float32)
            looked = looked + jnp.dot(pieces_ref[2], onehot, preferred_element_type=jnp.float32)
            softening = jnp.zeros((1, CHUNK), jnp.float32)
            for slip in range(SLIPS):
                active = ((codes >> slip) & 1).astype(jnp.float32)
                softening = softening + active * looked[1 + slip : 2 + slip, :]
            out_ref[0, plane : plane + 1, pl.ds(at, CHUNK)] = looked[0:1, :] / (1.0 + softening)
        return carry

    lax.fori_loop(0, codes_ref.shape[2] // CHUNK, chunk, 0)
    del rows


def stiffness(table, slip_code, grain_id):
    high = lax.reduce_precision(table, exponent_bits=8, mantissa_bits=7)
    rest = table - high
    middle = lax.reduce_precision(rest, exponent_bits=8, mantissa_bits=7)
    low = rest - middle
    pieces = jnp.stack([high, middle, low]).astype(jnp.bfloat16)
    pieces = jnp.pad(pieces, ((0, 0), (0, 16 - table.shape[0]), (0, 0)))
    rves, planes, cells = slip_code.shape
    block = pl.BlockSpec((1, planes, cells), lambda r: (r, 0, 0))
    return pl.pallas_call(
        stiffness_kernel,
        grid=(rves,),
        in_specs=[pl.BlockSpec(pieces.shape, lambda r: (0, 0, 0)), block, block],
        out_specs=block,
        out_shape=jax.ShapeDtypeStruct(slip_code.shape, jnp.float32),
    )(pieces, slip_code, grain_id)


def shift_cells(field, step):
    filler = jnp.zeros(field.shape[:-1] + (abs(step),), field.dtype)
    if step > 0:
        return jnp.concatenate([field[..., step:], filler], -1)
    return jnp.concatenate([filler, field[..., :step]], -1)


def local_dot(first, second):
    return jnp.sum(first * second, axis=(1, 2, 3))


def shards(macro_adjoint, slip_code, grain_id, grain_modulus, slip_softening, rve_spot):
    rve_count = slip_code.shape[0]
    cells = slip_code.shape[2]
    spot_count = macro_adjoint.shape[0] * lax.axis_size("hot")
    column = jnp.arange(cells) % RES
    upper_mask = (column != RES - 1).astype(jnp.float32)
    lower_mask = (column != 0).astype(jnp.float32)
    table = jnp.concatenate([grain_modulus[None, :], slip_softening.T], 0)

    spot_onehot = (rve_spot[:, None] == jnp.arange(spot_count)[None, :]).astype(jnp.float32)
    parts, hot_me = axis_gather(macro_adjoint, "hot")
    if hot_me is None:
        all_strains = parts[0]
    else:
        local = macro_adjoint.shape[0]
        ordered = []
        for j in range(len(parts)):
            pick = [(hot_me ^ o) == j for o in range(len(parts))]
            block = parts[0]
            for o in range(1, len(parts)):
                block = jnp.where(pick[o], parts[o], block)
            ordered.append(block)
        all_strains = jnp.concatenate(ordered, 0)
    strains = jnp.dot(
        spot_onehot,
        all_strains,
        precision=lax.Precision.HIGHEST,
        preferred_element_type=jnp.float32,
    )
    stiff_slabs = stiffness(table, slip_code, grain_id)
    stiff = lax.all_to_all(stiff_slabs, "xc", 0, 1, tiled=True)
    mine = lax.axis_index("xc")
    strains = lax.dynamic_slice_in_dim(strains, mine, 1, 0)
    padded = padded_2(stiff, (("yb", 1),), 2)
    wide = padded[:, 1:-1]
    wide_xup, wide_xdn = padded[:, 2:], padded[:, :-2]
    wide_yup, wide_ydn = shift_cells(wide, RES), shift_cells(wide, -RES)
    wide_zup, wide_zdn = shift_cells(wide, 1) * upper_mask, shift_cells(wide, -1) * lower_mask

    def inner(planes):
        return planes[:, 1:-1]

    near_xup, near_xdn = inner(wide_xup), inner(wide_xdn)
    near_yup, near_ydn = inner(wide_yup), inner(wide_ydn)
    near_zup, near_zdn = inner(wide_zup), inner(wide_zdn)
    face_xup = 0.5 * (stiff + near_xup)
    face_xdn = 0.5 * (stiff + near_xdn)
    face_yup = 0.5 * (stiff + near_yup)
    face_ydn = 0.5 * (stiff + near_ydn)
    face_zup = 0.5 * (stiff + near_zup)
    face_zdn = 0.5 * (stiff + near_zdn)
    diagonal_sum = (mass_term + face_xup + face_xdn + face_yup + face_ydn + face_zup + face_zdn)[
        :, None
    ]
    wide_gradients = [
        0.5 * (wide_xup - wide_xdn),
        0.5 * (wide_yup - wide_ydn),
        0.5 * (wide_zup - wide_zdn),
    ]
    gradients = [inner(g) for g in wide_gradients]
    tensor = [
        [strains[:, 0], strains[:, 5], strains[:, 4]],
        [strains[:, 5], strains[:, 1], strains[:, 3]],
        [strains[:, 4], strains[:, 3], strains[:, 2]],
    ]
    wide_source = jnp.stack(
        [
            wide_gradients[0] * tensor[comp][0][:, None, None]
            + wide_gradients[1] * tensor[comp][1][:, None, None]
            + wide_gradients[2] * tensor[comp][2][:, None, None]
            for comp in range(3)
        ],
        1,
    )
    source = wide_source[:, :, 1:-1]
    plane_block = lax.axis_index("yb")
    source_edges = jnp.concatenate(
        [
            jnp.where(plane_block != 0, wide_source[:, :, :1], 0.0),
            jnp.where(plane_block != lax.axis_size("yb") - 1, wide_source[:, :, -1:], 0.0),
        ],
        2,
    )

    def expand(values):
        return values[:, None, None, None]

    def boundary_planes(value):
        size = lax.axis_size("yb")
        up = [(i, i + 1) for i in range(size - 1)]
        down = [(i + 1, i) for i in range(size - 1)]
        before = lax.ppermute(value[:, :, -1:], "yb", up)
        after = lax.ppermute(value[:, :, :1], "yb", down)
        return jnp.concatenate([before, after], 2)

    def operate(direction, edges):
        wide = jnp.concatenate([edges[:, :, :1], direction, edges[:, :, 1:]], 2)
        return (
            diagonal_sum * direction
            - face_xup[:, None] * wide[:, :, 2:]
            - face_xdn[:, None] * wide[:, :, :-2]
            - face_yup[:, None] * shift_cells(direction, RES)
            - face_ydn[:, None] * shift_cells(direction, -RES)
            - face_zup[:, None] * (shift_cells(direction, 1) * upper_mask)
            - face_zdn[:, None] * (shift_cells(direction, -1) * lower_mask)
        )

    answer = jnp.zeros_like(source)
    residual = source
    direction = source
    residual_edges = source_edges
    direction_edges = residual_edges
    for step in range(ITERS):
        image = operate(direction, direction_edges)
        last = step + 1 == ITERS
        if not last:
            image_edges = boundary_planes(image)
        terms = [
            local_dot(direction, image),
            local_dot(residual, residual),
            local_dot(residual, image),
            local_dot(image, image),
        ]
        if last:
            for held in (answer, direction):
                terms += [
                    jnp.sum(held[:, comp] * gradients[other], axis=(1, 2))
                    for comp in range(3)
                    for other in range(3)
                ]
            terms.append(jnp.sum(stiff, axis=(1, 2)))
        local = jnp.stack(terms, -1)
        if last:
            sums = axis_sum(local, "yb")
            norm_now = sums[:, 1]
            alpha = norm_now / sums[:, 0]
        else:
            lanes = axis_sum(jnp.broadcast_to(local[:, :, None], local.shape + (128,)), "yb")
            lane_alpha = lanes[:, 1] / lanes[:, 0]
            lane_next = lanes[:, 1] - 2.0 * lane_alpha * lanes[:, 2] + lane_alpha * lane_alpha * lanes[:, 3]
            lane_beta = lane_next / lanes[:, 1]
            alpha = lane_alpha[:, 0]
        answer = answer + expand(alpha) * direction
        if last:
            break
        beta = expand(lane_beta[:, 0])
        residual = residual - expand(alpha) * image
        residual_edges = residual_edges - expand(alpha) * image_edges
        direction = residual + beta * direction
        direction_edges = residual_edges + beta * direction_edges
    volume = float(RES**3)
    moments = sums[:, 4:13] + alpha[:, None] * sums[:, 13:22]
    pair_sum = jnp.take(moments, jnp.array([0, 4, 8, 5, 2, 1]), axis=1) + jnp.take(
        moments, jnp.array([0, 4, 8, 7, 6, 3]), axis=1
    )
    rve_one = sums[:, 22:23] / volume * strains - 0.5 * pair_sum / volume
    per_spot = float(rve_count * lax.axis_size("hot") // spot_count)
    placed = (jnp.arange(rve_count)[:, None] == mine).astype(jnp.float32) * rve_one
    rve_totals = axis_sum(placed, "xc")
    spot_local = jnp.dot(
        spot_onehot.T,
        rve_totals,
        precision=lax.Precision.HIGHEST,
        preferred_element_type=jnp.float32,
    )
    owned = axis_reduce_scatter(spot_local, "hot")
    return (owned / per_spot, lax.all_to_all(answer, "xc", 2, 0, tiled=True))


def solution(mesh):
    hot, dom = mesh.shape["hot"], mesh.shape["dom"]
    rves_here = RVES // hot
    grouped = Mesh(mesh.devices.reshape(hot, dom // rves_here, rves_here), ("hot", "yb", "xc"))
    return jax.shard_map(
        shards,
        mesh=grouped,
        in_specs=(
            P("hot", None),
            P("hot", ("yb", "xc"), None),
            P("hot", ("yb", "xc"), None),
            P(),
            P(),
            P("hot"),
        ),
        out_specs=(P("hot", None), P("hot", None, ("yb", "xc"), None)),
        check_vma=False,
    )
```

```python
import jax
import jax.numpy as jnp
from jax import lax
from jax.experimental import pallas as pl
from jax.sharding import Mesh, PartitionSpec as P

RES = 64
SLIPS = 12
GRAINS = 64
ITERS = 8
RVES = 32


mass_term = 0.02


def padded_2(value, sides, width):
    for axis, dim in sides:
        devices, length = (lax.axis_size(axis), value.shape[dim])
        up = [(i, (i + 1) % devices) for i in range(devices - 1)]
        down = [(j, i) for i, j in up]
        last = lax.slice_in_dim(value, length - width, length, axis=dim)
        leading = lax.slice_in_dim(value, 0, width, axis=dim)
        before = lax.ppermute(last, axis, up)
        after = lax.ppermute(leading, axis, down)
        value = jnp.concatenate([before, value, after], axis=dim)
    return value


def xor_groups(size):
    bits = size.bit_length() - 1
    if size != 1 << bits:
        return None
    groups = [(0, 1)] if bits % 2 else []
    lo = bits % 2
    while lo < bits:
        groups.append((lo, 2))
        lo += 2
    return groups


def tree_sum(vals, nb):
    cur = dict(vals)
    for level in range(nb):
        cur = {o: v + cur[o | (1 << level)] for o, v in cur.items() if not o & (1 << level)}
    return cur[0]


def axis_sum(value, axis):
    size = lax.axis_size(axis)
    groups = xor_groups(size)
    if groups is None:
        return lax.psum(value, axis)
    for lo, nb in groups:
        vals = {0: value}
        for o in range(1, 1 << nb):
            mask = o << lo
            vals[o] = lax.ppermute(value, axis, [(i, i ^ mask) for i in range(size)])
        value = tree_sum(vals, nb)
    return value


def axis_gather(value, axis):
    size = lax.axis_size(axis)
    if xor_groups(size) is None:
        return [lax.all_gather(value, axis, axis=0, tiled=True)], None
    parts = [value] + [
        lax.ppermute(value, axis, [(i, i ^ o) for i in range(size)]) for o in range(1, size)
    ]
    return parts, lax.axis_index(axis)


def axis_reduce_scatter(value, axis):
    size = lax.axis_size(axis)
    if xor_groups(size) is None:
        return lax.psum_scatter(value, axis, scatter_dimension=0, tiled=True)
    me = lax.axis_index(axis)
    block = value.shape[0] // size
    nb = size.bit_length() - 1
    vals = {0: lax.dynamic_slice_in_dim(value, me * block, block, 0)}
    for o in range(1, size):
        wanted = lax.dynamic_slice_in_dim(value, (me ^ o) * block, block, 0)
        vals[o] = lax.ppermute(wanted, axis, [(i, i ^ o) for i in range(size)])
    return tree_sum(vals, nb)


CHUNK = 512


def stiffness_kernel(pieces_ref, codes_ref, grains_ref, out_ref):
    rows = pieces_ref.shape[1]

    def chunk(c, carry):
        at = pl.multiple_of(c * CHUNK, CHUNK)
        for plane in range(codes_ref.shape[1]):
            grains = grains_ref[0, plane : plane + 1, pl.ds(at, CHUNK)]
            codes = codes_ref[0, plane : plane + 1, pl.ds(at, CHUNK)]
            onehot = (lax.broadcasted_iota(jnp.int32, (GRAINS, CHUNK), 0) == grains).astype(jnp.bfloat16)
            looked = jnp.dot(pieces_ref[0], onehot, preferred_element_type=jnp.float32)
            looked = looked + jnp.dot(pieces_ref[1], onehot, preferred_element_type=jnp.float32)
            looked = looked + jnp.dot(pieces_ref[2], onehot, preferred_element_type=jnp.float32)
            softening = jnp.zeros((1, CHUNK), jnp.float32)
            for slip in range(SLIPS):
                active = ((codes >> slip) & 1).astype(jnp.float32)
                softening = softening + active * looked[1 + slip : 2 + slip, :]
            out_ref[0, plane : plane + 1, pl.ds(at, CHUNK)] = looked[0:1, :] / (1.0 + softening)
        return carry

    lax.fori_loop(0, codes_ref.shape[2] // CHUNK, chunk, 0)
    del rows


def stiffness(table, slip_code, grain_id):
    high = lax.reduce_precision(table, exponent_bits=8, mantissa_bits=7)
    rest = table - high
    middle = lax.reduce_precision(rest, exponent_bits=8, mantissa_bits=7)
    low = rest - middle
    pieces = jnp.stack([high, middle, low]).astype(jnp.bfloat16)
    pieces = jnp.pad(pieces, ((0, 0), (0, 16 - table.shape[0]), (0, 0)))
    rves, planes, cells = slip_code.shape
    block = pl.BlockSpec((1, planes, cells), lambda r: (r, 0, 0))
    return pl.pallas_call(
        stiffness_kernel,
        grid=(rves,),
        in_specs=[pl.BlockSpec(pieces.shape, lambda r: (0, 0, 0)), block, block],
        out_specs=block,
        out_shape=jax.ShapeDtypeStruct(slip_code.shape, jnp.float32),
    )(pieces, slip_code, grain_id)


def shift_cells(field, step):
    filler = jnp.zeros(field.shape[:-1] + (abs(step),), field.dtype)
    if step > 0:
        return jnp.concatenate([field[..., step:], filler], -1)
    return jnp.concatenate([filler, field[..., :step]], -1)


def local_dot(first, second):
    return jnp.sum(first * second, axis=(1, 2, 3))


def shards(macro_adjoint, slip_code, grain_id, grain_modulus, slip_softening, rve_spot):
    rve_count = slip_code.shape[0]
    cells = slip_code.shape[2]
    spot_count = macro_adjoint.shape[0] * lax.axis_size("hot")
    column = jnp.arange(cells) % RES
    upper_mask = (column != RES - 1).astype(jnp.float32)
    lower_mask = (column != 0).astype(jnp.float32)
    table = jnp.concatenate([grain_modulus[None, :], slip_softening.T], 0)

    def stiff_one(inputs):
        codes, grain_cells = inputs
        flat_codes = codes.reshape(-1)
        flat_grains = grain_cells.reshape(-1)
        onehot = (jnp.arange(GRAINS)[:, None] == flat_grains[None, :]).astype(jnp.float32)
        looked = jnp.dot(
            table, onehot, precision=lax.Precision.HIGHEST, preferred_element_type=jnp.float32
        )
        softening = jnp.zeros(flat_codes.shape, jnp.float32)
        for slip in range(SLIPS):
            active = (flat_codes // 2**slip % 2).astype(jnp.float32)
            softening = softening + active * looked[1 + slip]
        return (looked[0] / (1.0 + softening)).reshape(codes.shape)

    spot_onehot = (rve_spot[:, None] == jnp.arange(spot_count)[None, :]).astype(jnp.float32)
    parts, hot_me = axis_gather(macro_adjoint, "hot")
    if hot_me is None:
        all_strains = parts[0]
    else:
        local = macro_adjoint.shape[0]
        ordered = []
        for j in range(len(parts)):
            pick = [(hot_me ^ o) == j for o in range(len(parts))]
            block = parts[0]
            for o in range(1, len(parts)):
                block = jnp.where(pick[o], parts[o], block)
            ordered.append(block)
        all_strains = jnp.concatenate(ordered, 0)
    strains = jnp.dot(
        spot_onehot,
        all_strains,
        precision=lax.Precision.HIGHEST,
        preferred_element_type=jnp.float32,
    )
    stiff_slabs = stiffness(table, slip_code, grain_id)
    stiff = lax.all_to_all(stiff_slabs, "xc", 0, 1, tiled=True)
    mine = lax.axis_index("xc")
    strains = lax.dynamic_slice_in_dim(strains, mine, 1, 0)
    padded = padded_2(stiff, (("yb", 1),), 2)
    wide = padded[:, 1:-1]
    wide_xup, wide_xdn = padded[:, 2:], padded[:, :-2]
    wide_yup, wide_ydn = shift_cells(wide, RES), shift_cells(wide, -RES)
    wide_zup, wide_zdn = shift_cells(wide, 1) * upper_mask, shift_cells(wide, -1) * lower_mask

    def inner(planes):
        return planes[:, 1:-1]

    near_xup, near_xdn = inner(wide_xup), inner(wide_xdn)
    near_yup, near_ydn = inner(wide_yup), inner(wide_ydn)
    near_zup, near_zdn = inner(wide_zup), inner(wide_zdn)
    face_xup = 0.5 * (stiff + near_xup)
    face_xdn = 0.5 * (stiff + near_xdn)
    face_yup = 0.5 * (stiff + near_yup)
    face_ydn = 0.5 * (stiff + near_ydn)
    face_zup = 0.5 * (stiff + near_zup)
    face_zdn = 0.5 * (stiff + near_zdn)
    diagonal_sum = (mass_term + face_xup + face_xdn + face_yup + face_ydn + face_zup + face_zdn)[
        :, None
    ]
    wide_gradients = [
        0.5 * (wide_xup - wide_xdn),
        0.5 * (wide_yup - wide_ydn),
        0.5 * (wide_zup - wide_zdn),
    ]
    gradients = [inner(g) for g in wide_gradients]
    tensor = [
        [strains[:, 0], strains[:, 5], strains[:, 4]],
        [strains[:, 5], strains[:, 1], strains[:, 3]],
        [strains[:, 4], strains[:, 3], strains[:, 2]],
    ]
    wide_source = jnp.stack(
        [
            wide_gradients[0] * tensor[comp][0][:, None, None]
            + wide_gradients[1] * tensor[comp][1][:, None, None]
            + wide_gradients[2] * tensor[comp][2][:, None, None]
            for comp in range(3)
        ],
        1,
    )
    source = wide_source[:, :, 1:-1]
    plane_block = lax.axis_index("yb")
    source_edges = jnp.concatenate(
        [
            jnp.where(plane_block != 0, wide_source[:, :, :1], 0.0),
            jnp.where(plane_block != lax.axis_size("yb") - 1, wide_source[:, :, -1:], 0.0),
        ],
        2,
    )

    def expand(values):
        return values[:, None, None, None]

    def boundary_planes(value):
        size = lax.axis_size("yb")
        up = [(i, i + 1) for i in range(size - 1)]
        down = [(i + 1, i) for i in range(size - 1)]
        before = lax.ppermute(value[:, :, -1:], "yb", up)
        after = lax.ppermute(value[:, :, :1], "yb", down)
        return jnp.concatenate([before, after], 2)

    def operate(direction, edges):
        wide = jnp.concatenate([edges[:, :, :1], direction, edges[:, :, 1:]], 2)
        return (
            diagonal_sum * direction
            - face_xup[:, None] * wide[:, :, 2:]
            - face_xdn[:, None] * wide[:, :, :-2]
            - face_yup[:, None] * shift_cells(direction, RES)
            - face_ydn[:, None] * shift_cells(direction, -RES)
            - face_zup[:, None] * (shift_cells(direction, 1) * upper_mask)
            - face_zdn[:, None] * (shift_cells(direction, -1) * lower_mask)
        )

    answer = jnp.zeros_like(source)
    residual = source
    direction = source
    residual_edges = source_edges
    direction_edges = residual_edges
    for step in range(ITERS):
        image = operate(direction, direction_edges)
        last = step + 1 == ITERS
        if not last:
            image_edges = boundary_planes(image)
        terms = [
            local_dot(direction, image),
            local_dot(residual, residual),
            local_dot(residual, image),
            local_dot(image, image),
        ]
        if last:
            for held in (answer, direction):
                terms += [
                    jnp.sum(held[:, comp] * gradients[other], axis=(1, 2))
                    for comp in range(3)
                    for other in range(3)
                ]
            terms.append(jnp.sum(stiff, axis=(1, 2)))
        local = jnp.stack(terms, -1)
        if last:
            lanes = axis_sum(jnp.broadcast_to(local[:, :, None], local.shape + (128,)), "yb")
            lane_alpha = lanes[:, 1] / lanes[:, 0]
            sums = lanes[:, :, 0]
            alpha = lane_alpha[:, 0]
        else:
            lanes = axis_sum(jnp.broadcast_to(local[:, :, None], local.shape + (128,)), "yb")
            lane_alpha = lanes[:, 1] / lanes[:, 0]
            lane_next = lanes[:, 1] - 2.0 * lane_alpha * lanes[:, 2] + lane_alpha * lane_alpha * lanes[:, 3]
            lane_beta = lane_next / lanes[:, 1]
            alpha = lane_alpha[:, 0]
        answer = answer + expand(alpha) * direction
        if last:
            break
        beta = expand(lane_beta[:, 0])
        residual = residual - expand(alpha) * image
        residual_edges = residual_edges - expand(alpha) * image_edges
        direction = residual + beta * direction
        direction_edges = residual_edges + beta * direction_edges
    volume = float(RES**3)
    moments = sums[:, 4:13] + alpha[:, None] * sums[:, 13:22]
    pair_sum = jnp.take(moments, jnp.array([0, 4, 8, 5, 2, 1]), axis=1) + jnp.take(
        moments, jnp.array([0, 4, 8, 7, 6, 3]), axis=1
    )
    rve_one = sums[:, 22:23] / volume * strains - 0.5 * pair_sum / volume
    per_spot = float(rve_count * lax.axis_size("hot") // spot_count)
    placed = (jnp.arange(rve_count)[:, None] == mine).astype(jnp.float32) * rve_one
    rve_totals = axis_sum(placed, "xc")
    spot_local = jnp.dot(
        spot_onehot.T,
        rve_totals,
        precision=lax.Precision.HIGHEST,
        preferred_element_type=jnp.float32,
    )
    owned = axis_reduce_scatter(spot_local, "hot")
    return (owned / per_spot, lax.all_to_all(answer, "xc", 2, 0, tiled=True))


def solution(mesh):
    hot, dom = mesh.shape["hot"], mesh.shape["dom"]
    rves_here = RVES // hot
    grouped = Mesh(mesh.devices.reshape(hot, dom // rves_here, rves_here), ("hot", "yb", "xc"))
    return jax.shard_map(
        shards,
        mesh=grouped,
        in_specs=(
            P("hot", None),
            P("hot", ("yb", "xc"), None),
            P("hot", ("yb", "xc"), None),
            P(),
            P(),
            P("hot"),
        ),
        out_specs=(P("hot", None), P("hot", None, ("yb", "xc"), None)),
        check_vma=False,
    )
```
